128 devices in a mesh: ha: 64 (over y, z, x), ta: 2 (over core).
Axes of the slice: x: 4, y: 4, z: 4, core: 2. Of those that a mesh axis runs over, the one named last changes fastest.
Arguments:
- features: bfloat16 [8, 64, 640, 128], P('ta', 'ha'), may hold values from -6 to 6
- cotangent: bfloat16 [8, 64, 640, 128], P('ta', 'ha'), may hold values from -6 to 6
- kernel: bfloat16 [3, 3, 3, 128, 128], replicated, may hold values from -0.109375 to 0.109375
Outputs:
- grad_features: bfloat16 [8, 64, 640, 128], P('ta', 'ha')
- grad_kernel: float32 [3456, 128], P(('ha', 'ta'))
The draws below stay inside these ranges and needn't reach their ends.
All inputs are finite; a program needn't handle non-finite values.
Results may differ from the reference program's by a relative error of at most 0.003.
Values may be sent and summed in bfloat16 or wider, within the bound.
No kernel may reach another device: no remote copies, remote signals or barrier semaphores. Data moves between devices by JAX's collectives and lax.ppermute only.
A program may use at most 128 MiB of HBM per device.

```python
import jax
import jax.numpy as jnp
from jax import lax

C = 128
TAPS = 27
WIDTH = 640
FRAMES = 8
HEIGHT = 64


def block_scale(stream_key, dims, shards, smallest, largest):
    level, own = 1.0, jax.random.fold_in(stream_key, 6)
    for position, blocks in shards:
        heights = jnp.exp(jax.random.uniform(jax.random.fold_in(own, position), (blocks,), jnp.float32, smallest / len(shards), largest / len(shards)))
        level = level * jnp.repeat(heights, dims[position] // blocks).reshape([-1 if axis == position else 1 for axis in range(len(dims))])
    return level


def normal_values(stream_key, extent, deviation, most, pieces=(), kind=jnp.bfloat16):
    result = jax.random.normal(stream_key, extent, jnp.float32) * deviation
    if len(pieces) > 0:
        result = block_scale(stream_key, extent, pieces, -0.22, 0.18) * result
    return jnp.clip(result, min=-most, max=most).astype(kind)


def setup_inputs(seed: int = 0) -> dict:
    arg_keys = jax.random.split(jax.random.key(seed), 4)
    return {
        "features": normal_values(arg_keys[0], (FRAMES, HEIGHT, WIDTH, C), 1.0, 6.0, ((0, 2), (1, 64))),
        "cotangent": normal_values(arg_keys[1], (FRAMES, HEIGHT, WIDTH, C), 1.0, 6.0, ((0, 2), (1, 64))),
        "kernel": normal_values(arg_keys[2], (3, 3, 3, C, C), (TAPS * C) ** -0.5, 0.109375),
    }


def reference(features, cotangent, kernel):
    frames, height, breadth, channels = features.shape
    values = features.astype(jnp.float32)
    active = jax.nn.silu(values).astype(jnp.bfloat16)
    act_pad = jnp.pad(active, ((2, 0), (1, 1), (1, 1), (0, 0)))
    cot_pad = jnp.pad(cotangent, ((0, 2), (1, 1), (1, 1), (0, 0)))
    cot_flat = cotangent.reshape(-1, channels)
    grad_input = jnp.zeros((frames * height * breadth, channels), jnp.float32)
    blocks = []
    for t_tap in range(3):
        for h_tap in range(3):
            cot_slab = jnp.concatenate([cot_pad[2 - t_tap:2 - t_tap + frames, 2 - h_tap:2 - h_tap + height, 2 - w_tap:2 - w_tap + breadth] for w_tap in range(3)], axis=-1).reshape(-1, 3 * channels)
            stacked = jnp.transpose(kernel[t_tap, h_tap], (0, 2, 1)).reshape(3 * channels, channels)
            grad_input = grad_input + jnp.dot(cot_slab, stacked, preferred_element_type=jnp.float32)
            act_slab = jnp.concatenate([act_pad[t_tap:t_tap + frames, h_tap:h_tap + height, w_tap:w_tap + breadth] for w_tap in range(3)], axis=-1).reshape(-1, 3 * channels)
            blocks.append(lax.dot_general(act_slab, cot_flat, (((0,), (0,)), ((), ())), preferred_element_type=jnp.float32))
    factor = float(frames * height * breadth) ** -0.5
    grad_kernel = jnp.concatenate(blocks, axis=0) * factor
    sigmoid_part = jax.nn.sigmoid(values)
    derivative = sigmoid_part * (1.0 + values * (1.0 - sigmoid_part))
    grad_features = (cotangent.astype(jnp.float32) + derivative * grad_input.reshape(features.shape)).astype(jnp.bfloat16)
    return grad_features, grad_kernel
```

```python
import jax
import jax.numpy as jnp
from jax import lax
from jax.sharding import PartitionSpec as P


def passed_along(block, axis, distance):
    devices = range(lax.axis_size(axis))
    route = [(i - distance, i) for i in devices if i - distance in devices]
    return lax.ppermute(block, axis, route)


def with_halo(x, sides, width):
    for axis, dim in sides:
        count, length = (lax.axis_size(axis), x.shape[dim])
        up = [(i, (i + 1) % count) for i in range(count - 1)]
        down = [(j, i) for i, j in up]
        last = lax.slice_in_dim(x, length - width, length, axis=dim)
        leading = lax.slice_in_dim(x, 0, width, axis=dim)
        before = lax.ppermute(last, axis, up)
        after = lax.ppermute(leading, axis, down)
        x = jnp.concatenate([before, x, after], axis=dim)
    return x


def body(features, cotangent, kernel):
    frames, height, breadth, channels = features.shape
    values = features.astype(jnp.float32)
    active = jax.nn.silu(values).astype(jnp.bfloat16)
    future = passed_along(cotangent[:2], "ta", -1)
    cot_ext = jnp.concatenate([cotangent, future], axis=0)
    cot_rows = with_halo(cot_ext, (("ha", 1),), 1)
    cot_pad = jnp.pad(cot_rows, ((0, 0), (0, 0), (1, 1), (0, 0)))
    cot_flat = cotangent.reshape(-1, channels)
    past = passed_along(active[-2:], "ta", 1)
    act_ext = jnp.concatenate([past, active], axis=0)
    act_rows = with_halo(act_ext, (("ha", 1),), 1)
    act_pad = jnp.pad(act_rows, ((0, 0), (0, 0), (1, 1), (0, 0)))
    grad_input = jnp.zeros((frames * height * breadth, channels), jnp.float32)
    blocks = []
    for t_tap in range(3):
        for h_tap in range(3):
            cot_slab = jnp.concatenate(
                [
                    cot_pad[
                        2 - t_tap : 2 - t_tap + frames,
                        2 - h_tap : 2 - h_tap + height,
                        2 - w_tap : 2 - w_tap + breadth,
                    ]
                    for w_tap in range(3)
                ],
                axis=-1,
            ).reshape(-1, 3 * channels)
            stacked = jnp.transpose(kernel[t_tap, h_tap], (0, 2, 1)).reshape(3 * channels, channels)
            grad_input = grad_input + jnp.dot(cot_slab, stacked, preferred_element_type=jnp.float32)
            act_slab = jnp.concatenate(
                [
                    act_pad[t_tap : t_tap + frames, h_tap : h_tap + height, w_tap : w_tap + breadth]
                    for w_tap in range(3)
                ],
                axis=-1,
            ).reshape(-1, 3 * channels)
            blocks.append(
                lax.dot_general(
                    act_slab, cot_flat, (((0,), (0,)), ((), ())), preferred_element_type=jnp.float32
                )
            )
    total_cells = frames * height * breadth * lax.axis_size("ha") * lax.axis_size("ta")
    factor = float(total_cells) ** (-0.5)
    term = jnp.concatenate(blocks, axis=0) * factor
    owners = lax.axis_size("ha") * lax.axis_size("ta")
    rows = term.shape[0] // owners
    padded = -(-rows // 8) * 8
    term = jnp.pad(term.reshape(owners, rows, channels), ((0, 0), (0, padded - rows), (0, 0)))
    grad_kernel = lax.psum_scatter(
        term.reshape(owners * padded, channels), ("ha", "ta"), scatter_dimension=0, tiled=True
    )[:rows]
    sigmoid_part = jax.nn.sigmoid(values)
    derivative = sigmoid_part * (1.0 + values * (1.0 - sigmoid_part))
    grad_features = (
        cotangent.astype(jnp.float32) + derivative * grad_input.reshape(features.shape)
    ).astype(jnp.bfloat16)
    return (grad_features, grad_kernel)


def solution(mesh):
    placed = (P("ta", "ha", None, None), P("ta", "ha", None, None), P())
    return jax.shard_map(
        body,
        mesh=mesh,
        in_specs=placed,
        out_specs=(P("ta", "ha", None, None), P(("ha", "ta"), None)),
        check_vma=False,
    )
```

```python
import jax
import jax.numpy as jnp
import numpy as np
from jax import lax
from jax.sharding import Mesh, NamedSharding
from jax.sharding import PartitionSpec as P

PHYSICAL = ("y", "z", "x")


def passed_along(block, axis, distance):
    devices = range(lax.axis_size(axis))
    route = [(i - distance, i) for i in devices if i - distance in devices]
    return lax.ppermute(block, axis, route)


def with_halo(x, sides, width):
    for axis, dim in sides:
        count, length = (lax.axis_size(axis), x.shape[dim])
        up = [(i, (i + 1) % count) for i in range(count - 1)]
        down = [(j, i) for i, j in up]
        last = lax.slice_in_dim(x, length - width, length, axis=dim)
        leading = lax.slice_in_dim(x, 0, width, axis=dim)
        before = lax.ppermute(last, axis, up)
        after = lax.ppermute(leading, axis, down)
        x = jnp.concatenate([before, x, after], axis=dim)
    return x


def body(features, cotangent, kernel):
    frames, height, breadth, channels = features.shape
    values = features.astype(jnp.float32)
    active = jax.nn.silu(values).astype(jnp.bfloat16)
    future = passed_along(cotangent[:2], "ta", -1)
    cot_ext = jnp.concatenate([cotangent, future], axis=0)
    cot_rows = with_halo(cot_ext, (("ha", 1),), 1)
    cot_pad = jnp.pad(cot_rows, ((0, 0), (0, 0), (1, 1), (0, 0)))
    cot_flat = cotangent.reshape(-1, channels)
    past = passed_along(active[-2:], "ta", 1)
    act_ext = jnp.concatenate([past, active], axis=0)
    act_rows = with_halo(act_ext, (("ha", 1),), 1)
    act_pad = jnp.pad(act_rows, ((0, 0), (0, 0), (1, 1), (0, 0)))
    grad_input = jnp.zeros((frames * height * breadth, channels), jnp.float32)
    blocks = []
    for t_tap in range(3):
        for h_tap in range(3):
            cot_slab = jnp.concatenate(
                [
                    cot_pad[
                        2 - t_tap : 2 - t_tap + frames,
                        2 - h_tap : 2 - h_tap + height,
                        2 - w_tap : 2 - w_tap + breadth,
                    ]
                    for w_tap in range(3)
                ],
                axis=-1,
            ).reshape(-1, 3 * channels)
            stacked = jnp.transpose(kernel[t_tap, h_tap], (0, 2, 1)).reshape(3 * channels, channels)
            grad_input = grad_input + jnp.dot(cot_slab, stacked, preferred_element_type=jnp.float32)
            act_slab = jnp.concatenate(
                [
                    act_pad[t_tap : t_tap + frames, h_tap : h_tap + height, w_tap : w_tap + breadth]
                    for w_tap in range(3)
                ],
                axis=-1,
            ).reshape(-1, 3 * channels)
            blocks.append(
                lax.dot_general(
                    act_slab, cot_flat, (((0,), (0,)), ((), ())), preferred_element_type=jnp.float32
                )
            )
    total_cells = frames * height * breadth * lax.axis_size("ha") * lax.axis_size("ta")
    factor = float(total_cells) ** (-0.5)
    term = jnp.concatenate(blocks, axis=0) * factor
    owners = lax.axis_size("ha") * lax.axis_size("ta")
    rows = term.shape[0] // owners
    padded = -(-rows // 8) * 8
    term = jnp.pad(term.reshape(owners, rows, channels), ((0, 0), (0, padded - rows), (0, 0)))
    sigmoid_part = jax.nn.sigmoid(values)
    derivative = sigmoid_part * (1.0 + values * (1.0 - sigmoid_part))
    grad_features = (
        cotangent.astype(jnp.float32) + derivative * grad_input.reshape(features.shape)
    ).astype(jnp.bfloat16)
    return (grad_features, term[None])


def physical_mesh(mesh):
    devices = mesh.devices
    coords = np.array([d.coords for d in devices.reshape(-1)])
    sizes = {"x": len(set(coords[:, 0])), "y": len(set(coords[:, 1])), "z": len(set(coords[:, 2]))}
    shape = tuple(sizes[a] for a in PHYSICAL) + (devices.shape[1],)
    grid = devices.reshape(shape)
    flat = np.array([d.coords for d in grid.reshape(-1)]).reshape(shape + (3,))
    want = np.stack(np.meshgrid(*[np.arange(n) for n in shape[:3]], indexing="ij"), -1)
    got = flat[..., 0, :][..., [1, 2, 0]]
    assert (got == want).all()
    return Mesh(grid, PHYSICAL + ("core",))


def reduce_blocks(term, order):
    rows = term.shape[2]
    part = term[0]
    for axis in order:
        part = lax.psum_scatter(part, axis, scatter_dimension=0, tiled=True)
    return part[0]


def solution(mesh):
    placed = (P("ta", "ha", None, None), P("ta", "ha", None, None), P())
    local = jax.shard_map(
        body,
        mesh=mesh,
        in_specs=placed,
        out_specs=(P("ta", "ha", None, None), P(("ha", "ta"))),
        check_vma=False,
    )
    grid = physical_mesh(mesh)
    order = ("core", "x", "z", "y")
    names = PHYSICAL + ("core",)
    sizes = [grid.shape[a] for a in names]

    def reorder(term):
        n, owners, padded, channels = term.shape
        t = term.reshape((n,) + tuple(sizes) + (padded, channels))
        perm = [0] + [1 + names.index(a) for a in order] + [5, 6]
        return t.transpose(perm).reshape(n, owners, padded, channels)

    def reduce_fn(term):
        rows = 27
        return reduce_blocks(term, order)

    rows_per = None

    def run(features, cotangent, kernel):
        grad_features, term = local(features, cotangent, kernel)
        channels = kernel.shape[-1]
        owners = term.shape[1]
        taps_rows = kernel.shape[0] * kernel.shape[1] * kernel.shape[2] * kernel.shape[3]
        rows = taps_rows // owners
        term = reorder(term)
        spec = P(names)
        part = jax.shard_map(
            lambda t: reduce_blocks(t, order)[:rows],
            mesh=grid,
            in_specs=spec,
            out_specs=P(names),
            check_vma=False,
        )(term)
        part = lax.with_sharding_constraint(part, NamedSharding(mesh, P(("ha", "ta"), None)))
        return grad_features, part

    return run
```

```python
import jax
import jax.numpy as jnp
from jax import lax
from jax.sharding import PartitionSpec as P


def passed_along(block, axis, distance):
    devices = range(lax.axis_size(axis))
    route = [(i - distance, i) for i in devices if i - distance in devices]
    return lax.ppermute(block, axis, route)


def with_halo(x, sides, width):
    for axis, dim in sides:
        count, length = (lax.axis_size(axis), x.shape[dim])
        up = [(i, (i + 1) % count) for i in range(count - 1)]
        down = [(j, i) for i, j in up]
        last = lax.slice_in_dim(x, length - width, length, axis=dim)
        leading = lax.slice_in_dim(x, 0, width, axis=dim)
        before = lax.ppermute(last, axis, up)
        after = lax.ppermute(leading, axis, down)
        x = jnp.concatenate([before, x, after], axis=dim)
    return x


def body(features, cotangent, kernel):
    frames, height, breadth, channels = features.shape
    values = features.astype(jnp.float32)
    active = jax.nn.silu(values).astype(jnp.bfloat16)
    future = passed_along(cotangent[:2], "ta", -1)
    cot_ext = jnp.concatenate([cotangent, future], axis=0)
    cot_rows = with_halo(cot_ext, (("ha", 1),), 1)
    cot_pad = jnp.pad(cot_rows, ((0, 0), (0, 0), (1, 1), (0, 0)))
    cot_flat = cotangent.reshape(-1, channels)
    past = passed_along(active[-2:], "ta", 1)
    act_ext = jnp.concatenate([past, active], axis=0)
    act_rows = with_halo(act_ext, (("ha", 1),), 1)
    act_pad = jnp.pad(act_rows, ((0, 0), (0, 0), (1, 1), (0, 0)))
    grad_input = jnp.zeros((frames * height * breadth, channels), jnp.float32)
    blocks = []
    for t_tap in range(3):
        for h_tap in range(3):
            cot_slab = jnp.concatenate(
                [
                    cot_pad[
                        2 - t_tap : 2 - t_tap + frames,
                        2 - h_tap : 2 - h_tap + height,
                        2 - w_tap : 2 - w_tap + breadth,
                    ]
                    for w_tap in range(3)
                ],
                axis=-1,
            ).reshape(-1, 3 * channels)
            stacked = jnp.transpose(kernel[t_tap, h_tap], (0, 2, 1)).reshape(3 * channels, channels)
            grad_input = grad_input + jnp.dot(cot_slab, stacked, preferred_element_type=jnp.float32)
            act_slab = jnp.concatenate(
                [
                    act_pad[t_tap : t_tap + frames, h_tap : h_tap + height, w_tap : w_tap + breadth]
                    for w_tap in range(3)
                ],
                axis=-1,
            ).reshape(-1, 3 * channels)
            blocks.append(
                lax.dot_general(
                    act_slab, cot_flat, (((0,), (0,)), ((), ())), preferred_element_type=jnp.float32
                )
            )
    total_cells = frames * height * breadth * lax.axis_size("ha") * lax.axis_size("ta")
    factor = float(total_cells) ** (-0.5)
    term = jnp.concatenate(blocks, axis=0) * factor
    total = lax.psum(term, ("ha", "ta"))
    rows = term.shape[0] // (lax.axis_size("ha") * lax.axis_size("ta"))
    owner = lax.axis_index("ha") * lax.axis_size("ta") + lax.axis_index("ta")
    grad_kernel = lax.dynamic_slice_in_dim(total, owner * rows, rows, axis=0)
    sigmoid_part = jax.nn.sigmoid(values)
    derivative = sigmoid_part * (1.0 + values * (1.0 - sigmoid_part))
    grad_features = (
        cotangent.astype(jnp.float32) + derivative * grad_input.reshape(features.shape)
    ).astype(jnp.bfloat16)
    return (grad_features, grad_kernel)


def solution(mesh):
    placed = (P("ta", "ha", None, None), P("ta", "ha", None, None), P())
    return jax.shard_map(
        body,
        mesh=mesh,
        in_specs=placed,
        out_specs=(P("ta", "ha", None, None), P(("ha", "ta"), None)),
        check_vma=False,
    )
```

```python
import jax
import jax.numpy as jnp
import numpy as np
from jax import lax
from jax.sharding import Mesh, NamedSharding
from jax.sharding import PartitionSpec as P

PHYSICAL = ("y", "z", "x")


def passed_along(block, axis, distance):
    devices = range(lax.axis_size(axis))
    route = [(i - distance, i) for i in devices if i - distance in devices]
    return lax.ppermute(block, axis, route)


def with_halo(x, sides, width):
    for axis, dim in sides:
        count, length = (lax.axis_size(axis), x.shape[dim])
        up = [(i, (i + 1) % count) for i in range(count - 1)]
        down = [(j, i) for i, j in up]
        last = lax.slice_in_dim(x, length - width, length, axis=dim)
        leading = lax.slice_in_dim(x, 0, width, axis=dim)
        before = lax.ppermute(last, axis, up)
        after = lax.ppermute(leading, axis, down)
        x = jnp.concatenate([before, x, after], axis=dim)
    return x


def body(features, cotangent, kernel):
    frames, height, breadth, channels = features.shape
    values = features.astype(jnp.float32)
    active = jax.nn.silu(values).astype(jnp.bfloat16)
    future = passed_along(cotangent[:2], "ta", -1)
    cot_ext = jnp.concatenate([cotangent, future], axis=0)
    cot_rows = with_halo(cot_ext, (("ha", 1),), 1)
    cot_pad = jnp.pad(cot_rows, ((0, 0), (0, 0), (1, 1), (0, 0)))
    cot_flat = cotangent.reshape(-1, channels)
    past = passed_along(active[-2:], "ta", 1)
    act_ext = jnp.concatenate([past, active], axis=0)
    act_rows = with_halo(act_ext, (("ha", 1),), 1)
    act_pad = jnp.pad(act_rows, ((0, 0), (0, 0), (1, 1), (0, 0)))
    grad_input = jnp.zeros((frames * height * breadth, channels), jnp.float32)
    blocks = []
    for t_tap in range(3):
        for h_tap in range(3):
            cot_slab = jnp.concatenate(
                [
                    cot_pad[
                        2 - t_tap : 2 - t_tap + frames,
                        2 - h_tap : 2 - h_tap + height,
                        2 - w_tap : 2 - w_tap + breadth,
                    ]
                    for w_tap in range(3)
                ],
                axis=-1,
            ).reshape(-1, 3 * channels)
            stacked = jnp.transpose(kernel[t_tap, h_tap], (0, 2, 1)).reshape(3 * channels, channels)
            grad_input = grad_input + jnp.dot(cot_slab, stacked, preferred_element_type=jnp.float32)
            act_slab = jnp.concatenate(
                [
                    act_pad[t_tap : t_tap + frames, h_tap : h_tap + height, w_tap : w_tap + breadth]
                    for w_tap in range(3)
                ],
                axis=-1,
            ).reshape(-1, 3 * channels)
            blocks.append(
                lax.dot_general(
                    act_slab, cot_flat, (((0,), (0,)), ((), ())), preferred_element_type=jnp.float32
                )
            )
    total_cells = frames * height * breadth * lax.axis_size("ha") * lax.axis_size("ta")
    factor = float(total_cells) ** (-0.5)
    term = jnp.concatenate(blocks, axis=0) * factor
    owners = lax.axis_size("ha") * lax.axis_size("ta")
    rows = term.shape[0] // owners
    padded = -(-rows // 8) * 8
    term = jnp.pad(term.reshape(owners, rows, channels), ((0, 0), (0, padded - rows), (0, 0)))
    sigmoid_part = jax.nn.sigmoid(values)
    derivative = sigmoid_part * (1.0 + values * (1.0 - sigmoid_part))
    grad_features = (
        cotangent.astype(jnp.float32) + derivative * grad_input.reshape(features.shape)
    ).astype(jnp.bfloat16)
    return (grad_features, term[None])


def physical_mesh(mesh):
    devices = mesh.devices
    coords = np.array([d.coords for d in devices.reshape(-1)])
    sizes = {"x": len(set(coords[:, 0])), "y": len(set(coords[:, 1])), "z": len(set(coords[:, 2]))}
    shape = tuple(sizes[a] for a in PHYSICAL) + (devices.shape[1],)
    grid = devices.reshape(shape)
    flat = np.array([d.coords for d in grid.reshape(-1)]).reshape(shape + (3,))
    want = np.stack(np.meshgrid(*[np.arange(n) for n in shape[:3]], indexing="ij"), -1)
    got = flat[..., 0, :][..., [1, 2, 0]]
    assert (got == want).all()
    return Mesh(grid, PHYSICAL + ("core",))


def reduce_blocks(term, order):
    rows = term.shape[2]
    part = term[0]
    for axis in order:
        count = lax.axis_size(axis)
        shaped = part.reshape((count, part.shape[0] // count) + part.shape[1:])
        part = lax.all_to_all(shaped, axis, 0, 0, tiled=True).sum(0)
    return part[0]


def solution(mesh):
    placed = (P("ta", "ha", None, None), P("ta", "ha", None, None), P())
    local = jax.shard_map(
        body,
        mesh=mesh,
        in_specs=placed,
        out_specs=(P("ta", "ha", None, None), P(("ha", "ta"))),
        check_vma=False,
    )
    grid = physical_mesh(mesh)
    order = ("core", "x", "z", "y")
    names = PHYSICAL + ("core",)
    sizes = [grid.shape[a] for a in names]

    def reorder(term):
        n, owners, padded, channels = term.shape
        t = term.reshape((n,) + tuple(sizes) + (padded, channels))
        perm = [0] + [1 + names.index(a) for a in order] + [5, 6]
        return t.transpose(perm).reshape(n, owners, padded, channels)

    def reduce_fn(term):
        rows = 27
        return reduce_blocks(term, order)

    rows_per = None

    def run(features, cotangent, kernel):
        grad_features, term = local(features, cotangent, kernel)
        channels = kernel.shape[-1]
        owners = term.shape[1]
        taps_rows = kernel.shape[0] * kernel.shape[1] * kernel.shape[2] * kernel.shape[3]
        rows = taps_rows // owners
        term = reorder(term)
        spec = P(names)
        part = jax.shard_map(
            lambda t: reduce_blocks(t, order)[:rows],
            mesh=grid,
            in_specs=spec,
            out_specs=P(names),
            check_vma=False,
        )(term)
        part = lax.with_sharding_constraint(part, NamedSharding(mesh, P(("ha", "ta"), None)))
        return grad_features, part

    return run
```

```python
import jax
import jax.numpy as jnp
import numpy as np
from jax import lax
from jax.sharding import Mesh, NamedSharding
from jax.sharding import PartitionSpec as P

PHYSICAL = ("y", "z", "x")


def passed_along(block, axis, distance):
    devices = range(lax.axis_size(axis))
    route = [(i - distance, i) for i in devices if i - distance in devices]
    return lax.ppermute(block, axis, route)


def with_halo(x, sides, width):
    for axis, dim in sides:
        count, length = (lax.axis_size(axis), x.shape[dim])
        up = [(i, (i + 1) % count) for i in range(count - 1)]
        down = [(j, i) for i, j in up]
        last = lax.slice_in_dim(x, length - width, length, axis=dim)
        leading = lax.slice_in_dim(x, 0, width, axis=dim)
        before = lax.ppermute(last, axis, up)
        after = lax.ppermute(leading, axis, down)
        x = jnp.concatenate([before, x, after], axis=dim)
    return x


def body(features, cotangent, kernel):
    frames, height, breadth, channels = features.shape
    values = features.astype(jnp.float32)
    active = jax.nn.silu(values).astype(jnp.bfloat16)
    future = passed_along(cotangent[:2], "ta", -1)
    cot_ext = jnp.concatenate([cotangent, future], axis=0)
    cot_rows = with_halo(cot_ext, (("ha", 1),), 1)
    cot_pad = jnp.pad(cot_rows, ((0, 0), (0, 0), (1, 1), (0, 0)))
    act_flat = active.reshape(-1, channels)
    grad_input = jnp.zeros((frames * height * breadth, channels), jnp.float32)
    blocks = []
    for t_tap in range(3):
        for h_tap in range(3):
            cot_slab = jnp.concatenate(
                [
                    cot_pad[
                        2 - t_tap : 2 - t_tap + frames,
                        2 - h_tap : 2 - h_tap + height,
                        2 - w_tap : 2 - w_tap + breadth,
                    ]
                    for w_tap in range(3)
                ],
                axis=-1,
            ).reshape(-1, 3 * channels)
            stacked = jnp.transpose(kernel[t_tap, h_tap], (0, 2, 1)).reshape(3 * channels, channels)
            grad_input = grad_input + jnp.dot(cot_slab, stacked, preferred_element_type=jnp.float32)
            paired = lax.dot_general(
                act_flat, cot_slab, (((0,), (0,)), ((), ())), preferred_element_type=jnp.float32
            )
            blocks.append(
                paired.reshape(channels, 3, channels).transpose(1, 0, 2).reshape(3 * channels, channels)
            )
    total_cells = frames * height * breadth * lax.axis_size("ha") * lax.axis_size("ta")
    factor = float(total_cells) ** (-0.5)
    term = jnp.concatenate(blocks, axis=0) * factor
    owners = lax.axis_size("ha") * lax.axis_size("ta")
    rows = term.shape[0] // owners
    padded = -(-rows // 8) * 8
    term = jnp.pad(term.reshape(owners, rows, channels), ((0, 0), (0, padded - rows), (0, 0)))
    sigmoid_part = jax.nn.sigmoid(values)
    derivative = sigmoid_part * (1.0 + values * (1.0 - sigmoid_part))
    grad_features = (
        cotangent.astype(jnp.float32) + derivative * grad_input.reshape(features.shape)
    ).astype(jnp.bfloat16)
    return (grad_features, term[None])


def physical_mesh(mesh):
    devices = mesh.devices
    coords = np.array([d.coords for d in devices.reshape(-1)])
    sizes = {"x": len(set(coords[:, 0])), "y": len(set(coords[:, 1])), "z": len(set(coords[:, 2]))}
    shape = tuple(sizes[a] for a in PHYSICAL) + (devices.shape[1],)
    grid = devices.reshape(shape)
    flat = np.array([d.coords for d in grid.reshape(-1)]).reshape(shape + (3,))
    want = np.stack(np.meshgrid(*[np.arange(n) for n in shape[:3]], indexing="ij"), -1)
    got = flat[..., 0, :][..., [1, 2, 0]]
    assert (got == want).all()
    return Mesh(grid, PHYSICAL + ("core",))


def reduce_blocks(term, order):
    rows = term.shape[2]
    part = term[0]
    for axis in order:
        count = lax.axis_size(axis)
        shaped = part.reshape((count, part.shape[0] // count) + part.shape[1:])
        part = lax.all_to_all(shaped, axis, 0, 0, tiled=True).sum(0)
    return part[0]


def solution(mesh):
    placed = (P("ta", "ha", None, None), P("ta", "ha", None, None), P())
    local = jax.shard_map(
        body,
        mesh=mesh,
        in_specs=placed,
        out_specs=(P("ta", "ha", None, None), P(("ha", "ta"))),
        check_vma=False,
    )
    grid = physical_mesh(mesh)
    order = ("core", "x", "z", "y")
    names = PHYSICAL + ("core",)
    sizes = [grid.shape[a] for a in names]

    def reorder(term):
        n, owners, padded, channels = term.shape
        t = term.reshape((n,) + tuple(sizes) + (padded, channels))
        perm = [0] + [1 + names.index(a) for a in order] + [5, 6]
        return t.transpose(perm).reshape(n, owners, padded, channels)

    def reduce_fn(term):
        rows = 27
        return reduce_blocks(term, order)

    rows_per = None

    def run(features, cotangent, kernel):
        grad_features, term = local(features, cotangent, kernel)
        channels = kernel.shape[-1]
        owners = term.shape[1]
        taps_rows = kernel.shape[0] * kernel.shape[1] * kernel.shape[2] * kernel.shape[3]
        rows = taps_rows // owners
        term = reorder(term)
        spec = P(names)
        part = jax.shard_map(
            lambda t: reduce_blocks(t, order)[:rows],
            mesh=grid,
            in_specs=spec,
            out_specs=P(names),
            check_vma=False,
        )(term)
        part = lax.with_sharding_constraint(part, NamedSharding(mesh, P(("ha", "ta"), None)))
        return grad_features, part

    return run
```

```python
import jax
import jax.numpy as jnp
import numpy as np
from jax import lax
from jax.sharding import Mesh, NamedSharding
from jax.sharding import PartitionSpec as P

PHYSICAL = ("y", "z", "x")


def passed_along(block, axis, distance):
    devices = range(lax.axis_size(axis))
    route = [(i - distance, i) for i in devices if i - distance in devices]
    return lax.ppermute(block, axis, route)


def with_halo(x, sides, width):
    for axis, dim in sides:
        count, length = (lax.axis_size(axis), x.shape[dim])
        up = [(i, (i + 1) % count) for i in range(count - 1)]
        down = [(j, i) for i, j in up]
        last = lax.slice_in_dim(x, length - width, length, axis=dim)
        leading = lax.slice_in_dim(x, 0, width, axis=dim)
        before = lax.ppermute(last, axis, up)
        after = lax.ppermute(leading, axis, down)
        x = jnp.concatenate([before, x, after], axis=dim)
    return x


def body(features, cotangent, kernel):
    frames, height, breadth, channels = features.shape
    values = features.astype(jnp.float32)
    active = jax.nn.silu(values).astype(jnp.bfloat16)
    future = passed_along(cotangent[:2], "ta", -1)
    cot_ext = jnp.concatenate([cotangent, future], axis=0)
    cot_rows = with_halo(cot_ext, (("ha", 1),), 1)
    taps = kernel.shape[:3]
    edges = ((0, 0), (0, 0), (1, 1))
    flipped = jnp.flip(kernel, (0, 1, 2))
    grad_input = lax.conv_general_dilated(
        cot_rows[None],
        flipped,
        (1, 1, 1),
        edges,
        dimension_numbers=("NDHWC", "DHWOI", "NDHWC"),
        preferred_element_type=jnp.float32,
    )[0]
    paired = lax.conv_general_dilated(
        cot_rows[..., None],
        active[:, :, :, None, :],
        (1, 1, 1),
        edges,
        dimension_numbers=("DHWNC", "DHWIO", "DHWCN"),
        preferred_element_type=jnp.float32,
    )
    total_cells = frames * height * breadth * lax.axis_size("ha") * lax.axis_size("ta")
    factor = float(total_cells) ** (-0.5)
    term = jnp.flip(paired, (0, 1, 2)).reshape(-1, channels) * factor
    owners = lax.axis_size("ha") * lax.axis_size("ta")
    rows = term.shape[0] // owners
    padded = -(-rows // 8) * 8
    term = jnp.pad(term.reshape(owners, rows, channels), ((0, 0), (0, padded - rows), (0, 0)))
    sigmoid_part = jax.nn.sigmoid(values)
    derivative = sigmoid_part * (1.0 + values * (1.0 - sigmoid_part))
    grad_features = (cotangent.astype(jnp.float32) + derivative * grad_input).astype(jnp.bfloat16)
    return (grad_features, term[None])


def physical_mesh(mesh):
    devices = mesh.devices
    coords = np.array([d.coords for d in devices.reshape(-1)])
    sizes = {"x": len(set(coords[:, 0])), "y": len(set(coords[:, 1])), "z": len(set(coords[:, 2]))}
    shape = tuple(sizes[a] for a in PHYSICAL) + (devices.shape[1],)
    grid = devices.reshape(shape)
    flat = np.array([d.coords for d in grid.reshape(-1)]).reshape(shape + (3,))
    want = np.stack(np.meshgrid(*[np.arange(n) for n in shape[:3]], indexing="ij"), -1)
    got = flat[..., 0, :][..., [1, 2, 0]]
    assert (got == want).all()
    return Mesh(grid, PHYSICAL + ("core",))


def reduce_blocks(term, order):
    rows = term.shape[2]
    part = term[0]
    for axis in order:
        count = lax.axis_size(axis)
        shaped = part.reshape((count, part.shape[0] // count) + part.shape[1:])
        part = lax.all_to_all(shaped, axis, 0, 0, tiled=True).sum(0)
    return part[0]


def solution(mesh):
    placed = (P("ta", "ha", None, None), P("ta", "ha", None, None), P())
    local = jax.shard_map(
        body,
        mesh=mesh,
        in_specs=placed,
        out_specs=(P("ta", "ha", None, None), P(("ha", "ta"))),
        check_vma=False,
    )
    grid = physical_mesh(mesh)
    order = ("core", "x", "z", "y")
    names = PHYSICAL + ("core",)
    sizes = [grid.shape[a] for a in names]

    def reorder(term):
        n, owners, padded, channels = term.shape
        t = term.reshape((n,) + tuple(sizes) + (padded, channels))
        perm = [0] + [1 + names.index(a) for a in order] + [5, 6]
        return t.transpose(perm).reshape(n, owners, padded, channels)

    def reduce_fn(term):
        rows = 27
        return reduce_blocks(term, order)

    rows_per = None

    def run(features, cotangent, kernel):
        grad_features, term = local(features, cotangent, kernel)
        channels = kernel.shape[-1]
        owners = term.shape[1]
        taps_rows = kernel.shape[0] * kernel.shape[1] * kernel.shape[2] * kernel.shape[3]
        rows = taps_rows // owners
        term = reorder(term)
        spec = P(names)
        part = jax.shard_map(
            lambda t: reduce_blocks(t, order)[:rows],
            mesh=grid,
            in_specs=spec,
            out_specs=P(names),
            check_vma=False,
        )(term)
        part = lax.with_sharding_constraint(part, NamedSharding(mesh, P(("ha", "ta"), None)))
        return grad_features, part

    return run
```

```python
import jax
import jax.numpy as jnp
import numpy as np
from jax import lax
from jax.sharding import Mesh, NamedSharding
from jax.sharding import PartitionSpec as P
from jax.experimental import pallas as pl
from jax.experimental.pallas import tpu as pltpu

PHYSICAL = ("y", "z", "x")


def passed_along(block, axis, distance):
    devices = range(lax.axis_size(axis))
    route = [(i - distance, i) for i in devices if i - distance in devices]
    return lax.ppermute(block, axis, route)


def with_halo(x, sides, width):
    for axis, dim in sides:
        count, length = (lax.axis_size(axis), x.shape[dim])
        up = [(i, (i + 1) % count) for i in range(count - 1)]
        down = [(j, i) for i, j in up]
        last = lax.slice_in_dim(x, length - width, length, axis=dim)
        leading = lax.slice_in_dim(x, 0, width, axis=dim)
        before = lax.ppermute(last, axis, up)
        after = lax.ppermute(leading, axis, down)
        x = jnp.concatenate([before, x, after], axis=dim)
    return x


def local_kernel(factor, cot_ref, kt_ref, a_ref, feat_ref, gf_ref, term_ref, z_ref):
    frames, breadth, channels = feat_ref.shape
    term_ref[...] = jnp.zeros_like(term_ref)
    rows = lax.broadcasted_iota(jnp.int32, (breadth, channels), 0)
    for t in range(frames):
        for i in range(3):
            for j in range(3):
                slab = cot_ref[t + 2 - i, 2 - j]
                part = jnp.dot(slab, kt_ref[i, j], preferred_element_type=jnp.float32)
                if i == 0 and j == 0:
                    z_ref[...] = part
                else:
                    z_ref[...] += part
                term_ref[i * 3 + j] += jnp.dot(a_ref[t], slab, preferred_element_type=jnp.float32)
        ahead = pltpu.roll(z_ref[:, 0:channels], breadth - 1, 0)
        behind = pltpu.roll(z_ref[:, 2 * channels : 3 * channels], 1, 0)
        grad_input = (
            jnp.where(rows == breadth - 1, 0.0, ahead)
            + z_ref[:, channels : 2 * channels]
            + jnp.where(rows == 0, 0.0, behind)
        )
        values = feat_ref[t].astype(jnp.float32)
        sigmoid_part = jax.nn.sigmoid(values)
        derivative = sigmoid_part * (1.0 + values * (1.0 - sigmoid_part))
        own = cot_ref[t, 1].astype(jnp.float32)
        gf_ref[t] = (own + derivative * grad_input).astype(gf_ref.dtype)
    term_ref[...] = term_ref[...] * factor


def local_grads(cot_rows, kt, a, feat, factor):
    frames, breadth, channels = feat.shape
    vmem = pl.BlockSpec(memory_space=pltpu.VMEM)
    flops = 2 * 2 * frames * 9 * breadth * channels * 3 * channels
    moved = 2 * (cot_rows.size + kt.size + a.size + 2 * feat.size) + 4 * 9 * 3 * channels * channels
    return pl.pallas_call(
        lambda *refs: local_kernel(factor, *refs),
        out_shape=(
            jax.ShapeDtypeStruct((frames, breadth, channels), jnp.bfloat16),
            jax.ShapeDtypeStruct((9, 3 * channels, channels), jnp.float32),
        ),
        in_specs=[vmem] * 4,
        out_specs=(vmem, vmem),
        scratch_shapes=[pltpu.VMEM((breadth, 3 * channels), jnp.float32)],
        compiler_params=pltpu.CompilerParams(vmem_limit_bytes=48 * 1024 * 1024),
        cost_estimate=pl.CostEstimate(flops=flops, bytes_accessed=moved, transcendentals=feat.size),
    )(cot_rows, kt, a, feat)


def local_inputs(features, cotangent, kernel, cot_rows):
    frames, height, breadth, channels = features.shape
    active = jax.nn.silu(features.astype(jnp.float32)).astype(jnp.bfloat16)
    wide = jnp.pad(active[:, 0], ((0, 0), (1, 1), (0, 0)))
    shifted = jnp.stack([wide[:, k : k + breadth] for k in range(3)], axis=1)
    a = shifted.transpose(0, 1, 3, 2).reshape(frames, 3 * channels, breadth)
    kt = kernel.transpose(0, 1, 4, 2, 3).reshape(3, 3, channels, 3 * channels)
    return cot_rows[:, :, 0], kt, a, features[:, 0]


def body(features, cotangent, kernel):
    frames, height, breadth, channels = features.shape
    future = passed_along(cotangent[:2], "ta", -1)
    cot_ext = jnp.concatenate([cotangent, future], axis=0)
    cot_rows = with_halo(cot_ext, (("ha", 1),), 1)
    total_cells = frames * height * breadth * lax.axis_size("ha") * lax.axis_size("ta")
    factor = float(total_cells) ** (-0.5)
    cot_in, kt, a, feat = local_inputs(features, cotangent, kernel, cot_rows[:, :, None])
    grad_features, term = local_grads(cot_in, kt, a, feat, factor)
    term = term.reshape(-1, channels)
    owners = lax.axis_size("ha") * lax.axis_size("ta")
    rows = term.shape[0] // owners
    padded = -(-rows // 8) * 8
    term = jnp.pad(term.reshape(owners, rows, channels), ((0, 0), (0, padded - rows), (0, 0)))
    return (grad_features[:, None], term[None])


def physical_mesh(mesh):
    devices = mesh.devices
    coords = np.array([d.coords for d in devices.reshape(-1)])
    sizes = {"x": len(set(coords[:, 0])), "y": len(set(coords[:, 1])), "z": len(set(coords[:, 2]))}
    shape = tuple(sizes[a] for a in PHYSICAL) + (devices.shape[1],)
    grid = devices.reshape(shape)
    flat = np.array([d.coords for d in grid.reshape(-1)]).reshape(shape + (3,))
    want = np.stack(np.meshgrid(*[np.arange(n) for n in shape[:3]], indexing="ij"), -1)
    got = flat[..., 0, :][..., [1, 2, 0]]
    assert (got == want).all()
    return Mesh(grid, PHYSICAL + ("core",))


def reduce_blocks(term, order):
    rows = term.shape[2]
    part = term[0]
    for axis in order:
        count = lax.axis_size(axis)
        shaped = part.reshape((count, part.shape[0] // count) + part.shape[1:])
        part = lax.all_to_all(shaped, axis, 0, 0, tiled=True).sum(0)
    return part[0]


def solution(mesh):
    placed = (P("ta", "ha", None, None), P("ta", "ha", None, None), P())
    local = jax.shard_map(
        body,
        mesh=mesh,
        in_specs=placed,
        out_specs=(P("ta", "ha", None, None), P(("ha", "ta"))),
        check_vma=False,
    )
    grid = physical_mesh(mesh)
    order = ("core", "x", "z", "y")
    names = PHYSICAL + ("core",)
    sizes = [grid.shape[a] for a in names]

    def reorder(term):
        n, owners, padded, channels = term.shape
        t = term.reshape((n,) + tuple(sizes) + (padded, channels))
        perm = [0] + [1 + names.index(a) for a in order] + [5, 6]
        return t.transpose(perm).reshape(n, owners, padded, channels)

    def reduce_fn(term):
        rows = 27
        return reduce_blocks(term, order)

    rows_per = None

    def run(features, cotangent, kernel):
        grad_features, term = local(features, cotangent, kernel)
        channels = kernel.shape[-1]
        owners = term.shape[1]
        taps_rows = kernel.shape[0] * kernel.shape[1] * kernel.shape[2] * kernel.shape[3]
        rows = taps_rows // owners
        term = reorder(term)
        spec = P(names)
        part = jax.shard_map(
            lambda t: reduce_blocks(t, order)[:rows],
            mesh=grid,
            in_specs=spec,
            out_specs=P(names),
            check_vma=False,
        )(term)
        part = lax.with_sharding_constraint(part, NamedSharding(mesh, P(("ha", "ta"), None)))
        return grad_features, part

    return run
```

```python
import jax
import jax.numpy as jnp
import numpy as np
from jax import lax
from jax.sharding import Mesh, NamedSharding
from jax.sharding import PartitionSpec as P
from jax.experimental import pallas as pl
from jax.experimental.pallas import tpu as pltpu

PHYSICAL = ("y", "z", "x")


def passed_along(block, axis, distance):
    devices = range(lax.axis_size(axis))
    route = [(i - distance, i) for i in devices if i - distance in devices]
    return lax.ppermute(block, axis, route)


def with_halo(x, sides, width):
    for axis, dim in sides:
        count, length = (lax.axis_size(axis), x.shape[dim])
        up = [(i, (i + 1) % count) for i in range(count - 1)]
        down = [(j, i) for i, j in up]
        last = lax.slice_in_dim(x, length - width, length, axis=dim)
        leading = lax.slice_in_dim(x, 0, width, axis=dim)
        before = lax.ppermute(last, axis, up)
        after = lax.ppermute(leading, axis, down)
        x = jnp.concatenate([before, x, after], axis=dim)
    return x


def local_kernel(factor, cot_ref, kt_ref, a_ref, feat_ref, gf_ref, term_ref, z_ref):
    frames, breadth, channels = feat_ref.shape
    term_ref[...] = jnp.zeros_like(term_ref)
    rows = lax.broadcasted_iota(jnp.int32, (breadth, channels), 0)
    for t in range(frames):
        for i in range(3):
            for j in range(3):
                slab = cot_ref[t + 2 - i, 2 - j]
                part = jnp.dot(slab, kt_ref[i, j], preferred_element_type=jnp.float32)
                if i == 0 and j == 0:
                    z_ref[...] = part
                else:
                    z_ref[...] += part
                term_ref[i * 3 + j] += jnp.dot(a_ref[t], slab, preferred_element_type=jnp.float32)
        ahead = pltpu.roll(z_ref[:, 0:channels], breadth - 1, 0)
        behind = pltpu.roll(z_ref[:, 2 * channels : 3 * channels], 1, 0)
        grad_input = (
            jnp.where(rows == breadth - 1, 0.0, ahead)
            + z_ref[:, channels : 2 * channels]
            + jnp.where(rows == 0, 0.0, behind)
        )
        values = feat_ref[t].astype(jnp.float32)
        sigmoid_part = jax.nn.sigmoid(values)
        derivative = sigmoid_part * (1.0 + values * (1.0 - sigmoid_part))
        own = cot_ref[t, 1].astype(jnp.float32)
        gf_ref[t] = (own + derivative * grad_input).astype(gf_ref.dtype)
    term_ref[...] = term_ref[...] * factor


def local_grads(cot_rows, kt, a, feat, factor):
    frames, breadth, channels = feat.shape
    vmem = pl.BlockSpec(memory_space=pltpu.VMEM)
    flops = 2 * 2 * frames * 9 * breadth * channels * 3 * channels
    moved = 2 * (cot_rows.size + kt.size + a.size + 2 * feat.size) + 4 * 9 * 3 * channels * channels
    return pl.pallas_call(
        lambda *refs: local_kernel(factor, *refs),
        out_shape=(
            jax.ShapeDtypeStruct((frames, breadth, channels), jnp.bfloat16),
            jax.ShapeDtypeStruct((9, 3 * channels, channels), jnp.float32),
        ),
        in_specs=[vmem] * 4,
        out_specs=(vmem, vmem),
        scratch_shapes=[pltpu.VMEM((breadth, 3 * channels), jnp.float32)],
        compiler_params=pltpu.CompilerParams(vmem_limit_bytes=48 * 1024 * 1024),
        cost_estimate=pl.CostEstimate(flops=flops, bytes_accessed=moved, transcendentals=feat.size),
    )(cot_rows, kt, a, feat)


def local_inputs(features, cotangent, kernel, cot_rows):
    frames, height, breadth, channels = features.shape
    active = jax.nn.silu(features.astype(jnp.float32)).astype(jnp.bfloat16)
    wide = jnp.pad(active[:, 0], ((0, 0), (1, 1), (0, 0)))
    shifted = jnp.stack([wide[:, k : k + breadth] for k in range(3)], axis=1)
    a = shifted.transpose(0, 1, 3, 2).reshape(frames, 3 * channels, breadth)
    kt = kernel.transpose(0, 1, 4, 2, 3).reshape(3, 3, channels, 3 * channels)
    return cot_rows[:, :, 0], kt, a, features[:, 0]


def body(features, cotangent, kernel):
    frames, height, breadth, channels = features.shape
    future = passed_along(cotangent[:2], "ta", -1)
    cot_ext = jnp.concatenate([cotangent, future], axis=0)
    cot_rows = with_halo(cot_ext, (("ha", 1),), 1)
    total_cells = frames * height * breadth * lax.axis_size("ha") * lax.axis_size("ta")
    factor = float(total_cells) ** (-0.5)
    cot_in, kt, a, feat = local_inputs(features, cotangent, kernel, cot_rows[:, :, None])
    grad_features, term = local_grads(cot_in, kt, a, feat, factor)
    term = term.reshape(-1, channels)
    owners = lax.axis_size("ha") * lax.axis_size("ta")
    rows = term.shape[0] // owners
    padded = -(-rows // 8) * 8
    term = jnp.pad(term.reshape(owners, rows, channels), ((0, 0), (0, padded - rows), (0, 0)))
    return (grad_features[:, None], term[None])


def physical_mesh(mesh):
    devices = mesh.devices
    coords = np.array([d.coords for d in devices.reshape(-1)])
    sizes = {"x": len(set(coords[:, 0])), "y": len(set(coords[:, 1])), "z": len(set(coords[:, 2]))}
    shape = tuple(sizes[a] for a in PHYSICAL) + (devices.shape[1],)
    grid = devices.reshape(shape)
    flat = np.array([d.coords for d in grid.reshape(-1)]).reshape(shape + (3,))
    want = np.stack(np.meshgrid(*[np.arange(n) for n in shape[:3]], indexing="ij"), -1)
    got = flat[..., 0, :][..., [1, 2, 0]]
    assert (got == want).all()
    return Mesh(grid, PHYSICAL + ("core",))


def reduce_blocks(term, order):
    rows = term.shape[2]
    part = term[0]
    for axis in order:
        count = lax.axis_size(axis)
        shaped = part.reshape((count, part.shape[0] // count) + part.shape[1:])
        part = lax.all_to_all(shaped, axis, 0, 0, tiled=True).sum(0)
    return part[0]


def solution(mesh):
    placed = (P("ta", "ha", None, None), P("ta", "ha", None, None), P())
    local = jax.shard_map(
        body,
        mesh=mesh,
        in_specs=placed,
        out_specs=(P("ta", "ha", None, None), P(("ha", "ta"))),
        check_vma=False,
    )
    grid = physical_mesh(mesh)
    order = ("core", "y", "z", "x")
    stages = ("core", PHYSICAL)
    names = PHYSICAL + ("core",)
    sizes = [grid.shape[a] for a in names]

    def reorder(term):
        n, owners, padded, channels = term.shape
        t = term.reshape((n,) + tuple(sizes) + (padded, channels))
        perm = [0] + [1 + names.index(a) for a in order] + [5, 6]
        return t.transpose(perm).reshape(n, owners, padded, channels)

    def reduce_fn(term):
        rows = 27
        return reduce_blocks(term, order)

    rows_per = None

    def run(features, cotangent, kernel):
        grad_features, term = local(features, cotangent, kernel)
        channels = kernel.shape[-1]
        owners = term.shape[1]
        taps_rows = kernel.shape[0] * kernel.shape[1] * kernel.shape[2] * kernel.shape[3]
        rows = taps_rows // owners
        term = reorder(term)
        spec = P(names)
        part = jax.shard_map(
            lambda t: reduce_blocks(t, stages)[:rows],
            mesh=grid,
            in_specs=spec,
            out_specs=P(names),
            check_vma=False,
        )(term)
        part = lax.with_sharding_constraint(part, NamedSharding(mesh, P(("ha", "ta"), None)))
        return grad_features, part

    return run
```

```python
import jax
import jax.numpy as jnp
import numpy as np
from jax import lax
from jax.sharding import Mesh, NamedSharding
from jax.sharding import PartitionSpec as P
from jax.experimental import pallas as pl
from jax.experimental.pallas import tpu as pltpu

PHYSICAL = ("y", "z", "x")


def passed_along(block, axis, distance):
    devices = range(lax.axis_size(axis))
    route = [(i - distance, i) for i in devices if i - distance in devices]
    return lax.ppermute(block, axis, route)


def with_halo(x, sides, width):
    for axis, dim in sides:
        count, length = (lax.axis_size(axis), x.shape[dim])
        up = [(i, (i + 1) % count) for i in range(count - 1)]
        down = [(j, i) for i, j in up]
        last = lax.slice_in_dim(x, length - width, length, axis=dim)
        leading = lax.slice_in_dim(x, 0, width, axis=dim)
        before = lax.ppermute(last, axis, up)
        after = lax.ppermute(leading, axis, down)
        x = jnp.concatenate([before, x, after], axis=dim)
    return x


def local_kernel(factor, own_ref, fut_ref, up_ref, down_ref, fwd_ref, kt_ref, a_ref, feat_ref, gf_ref, term_ref, z_ref):
    frames, breadth, channels = feat_ref.shape

    def slab(frame, row):
        if frame < frames:
            return (up_ref, own_ref, down_ref)[row][frame]
        if row == 1:
            return fut_ref[frame - frames]
        return fwd_ref[row // 2, frame - frames]

    term_ref[...] = jnp.zeros_like(term_ref)
    rows = lax.broadcasted_iota(jnp.int32, (breadth, channels), 0)
    for t in range(frames):
        for i in range(3):
            for j in range(3):
                piece = slab(t + 2 - i, 2 - j)
                part = jnp.dot(piece, kt_ref[i, j], preferred_element_type=jnp.float32)
                if i == 0 and j == 0:
                    z_ref[...] = part
                else:
                    z_ref[...] += part
                term_ref[i * 3 + j] += jnp.dot(a_ref[t], piece, preferred_element_type=jnp.float32)
        ahead = pltpu.roll(z_ref[:, 0:channels], breadth - 1, 0)
        behind = pltpu.roll(z_ref[:, 2 * channels : 3 * channels], 1, 0)
        grad_input = (
            jnp.where(rows == breadth - 1, 0.0, ahead)
            + z_ref[:, channels : 2 * channels]
            + jnp.where(rows == 0, 0.0, behind)
        )
        values = feat_ref[t].astype(jnp.float32)
        sigmoid_part = jax.nn.sigmoid(values)
        derivative = sigmoid_part * (1.0 + values * (1.0 - sigmoid_part))
        gf_ref[t] = (own_ref[t].astype(jnp.float32) + derivative * grad_input).astype(gf_ref.dtype)
    term_ref[...] = term_ref[...] * factor


def local_grads(pieces, kt, a, feat, factor):
    frames, breadth, channels = feat.shape
    vmem = pl.BlockSpec(memory_space=pltpu.VMEM)
    operands = tuple(pieces) + (kt, a, feat)
    flops = 2 * 2 * frames * 9 * breadth * channels * 3 * channels
    moved = sum(2 * x.size for x in operands) + 2 * feat.size + 4 * 9 * 3 * channels * channels
    return pl.pallas_call(
        lambda *refs: local_kernel(factor, *refs),
        out_shape=(
            jax.ShapeDtypeStruct((frames, breadth, channels), jnp.bfloat16),
            jax.ShapeDtypeStruct((9, 3 * channels, channels), jnp.float32),
        ),
        in_specs=[vmem] * len(operands),
        out_specs=(vmem, vmem),
        scratch_shapes=[pltpu.VMEM((breadth, 3 * channels), jnp.float32)],
        compiler_params=pltpu.CompilerParams(vmem_limit_bytes=48 * 1024 * 1024),
        cost_estimate=pl.CostEstimate(flops=flops, bytes_accessed=moved, transcendentals=feat.size),
    )(*operands)


def local_inputs(features, kernel):
    frames, height, breadth, channels = features.shape
    active = jax.nn.silu(features.astype(jnp.float32)).astype(jnp.bfloat16)
    wide = jnp.pad(active[:, 0], ((0, 0), (1, 1), (0, 0)))
    shifted = jnp.stack([wide[:, k : k + breadth] for k in range(3)], axis=1)
    a = shifted.transpose(0, 1, 3, 2).reshape(frames, 3 * channels, breadth)
    kt = kernel.transpose(0, 1, 4, 2, 3).reshape(3, 3, channels, 3 * channels)
    return kt, a, features[:, 0]


def row_neighbours(x, axis):
    count = lax.axis_size(axis)
    up = [(i, i + 1) for i in range(count - 1)]
    down = [(j, i) for i, j in up]
    return lax.ppermute(x, axis, up), lax.ppermute(x, axis, down)


def body(features, cotangent, kernel):
    frames, height, breadth, channels = features.shape
    own = cotangent[:, 0]
    future = passed_along(own[:2], "ta", -1)
    above, below = row_neighbours(own, "ha")
    forwarded = passed_along(jnp.stack([above[:2], below[:2]]), "ta", -1)
    total_cells = frames * height * breadth * lax.axis_size("ha") * lax.axis_size("ta")
    factor = float(total_cells) ** (-0.5)
    kt, a, feat = local_inputs(features, kernel)
    grad_features, term = local_grads((own, future, above, below, forwarded), kt, a, feat, factor)
    term = term.reshape(-1, channels)
    owners = lax.axis_size("ha") * lax.axis_size("ta")
    rows = term.shape[0] // owners
    padded = -(-rows // 8) * 8
    term = jnp.pad(term.reshape(owners, rows, channels), ((0, 0), (0, padded - rows), (0, 0)))
    return (grad_features[:, None], term[None])


def physical_mesh(mesh):
    devices = mesh.devices
    coords = np.array([d.coords for d in devices.reshape(-1)])
    sizes = {"x": len(set(coords[:, 0])), "y": len(set(coords[:, 1])), "z": len(set(coords[:, 2]))}
    shape = tuple(sizes[a] for a in PHYSICAL) + (devices.shape[1],)
    grid = devices.reshape(shape)
    flat = np.array([d.coords for d in grid.reshape(-1)]).reshape(shape + (3,))
    want = np.stack(np.meshgrid(*[np.arange(n) for n in shape[:3]], indexing="ij"), -1)
    got = flat[..., 0, :][..., [1, 2, 0]]
    assert (got == want).all()
    return Mesh(grid, PHYSICAL + ("core",))


def reduce_blocks(term, order):
    rows = term.shape[2]
    part = term[0]
    for axis in order:
        count = lax.axis_size(axis)
        shaped = part.reshape((count, part.shape[0] // count) + part.shape[1:])
        part = lax.all_to_all(shaped, axis, 0, 0, tiled=True).sum(0)
    return part[0]


def solution(mesh):
    placed = (P("ta", "ha", None, None), P("ta", "ha", None, None), P())
    local = jax.shard_map(
        body,
        mesh=mesh,
        in_specs=placed,
        out_specs=(P("ta", "ha", None, None), P(("ha", "ta"))),
        check_vma=False,
    )
    grid = physical_mesh(mesh)
    order = ("core", "y", "z", "x")
    stages = ("core", PHYSICAL)
    names = PHYSICAL + ("core",)
    sizes = [grid.shape[a] for a in names]

    def reorder(term):
        n, owners, padded, channels = term.shape
        t = term.reshape((n,) + tuple(sizes) + (padded, channels))
        perm = [0] + [1 + names.index(a) for a in order] + [5, 6]
        return t.transpose(perm).reshape(n, owners, padded, channels)

    def reduce_fn(term):
        rows = 27
        return reduce_blocks(term, order)

    rows_per = None

    def run(features, cotangent, kernel):
        grad_features, term = local(features, cotangent, kernel)
        channels = kernel.shape[-1]
        owners = term.shape[1]
        taps_rows = kernel.shape[0] * kernel.shape[1] * kernel.shape[2] * kernel.shape[3]
        rows = taps_rows // owners
        term = reorder(term)
        spec = P(names)
        part = jax.shard_map(
            lambda t: reduce_blocks(t, stages)[:rows],
            mesh=grid,
            in_specs=spec,
            out_specs=P(names),
            check_vma=False,
        )(term)
        part = lax.with_sharding_constraint(part, NamedSharding(mesh, P(("ha", "ta"), None)))
        return grad_features, part

    return run
```

```python
import jax
import jax.numpy as jnp
import numpy as np
from jax import lax
from jax.sharding import Mesh, NamedSharding
from jax.sharding import PartitionSpec as P
from jax.experimental import pallas as pl
from jax.experimental.pallas import tpu as pltpu

PHYSICAL = ("y", "z", "x")


def passed_along(block, axis, distance):
    devices = range(lax.axis_size(axis))
    route = [(i - distance, i) for i in devices if i - distance in devices]
    return lax.ppermute(block, axis, route)


def with_halo(x, sides, width):
    for axis, dim in sides:
        count, length = (lax.axis_size(axis), x.shape[dim])
        up = [(i, (i + 1) % count) for i in range(count - 1)]
        down = [(j, i) for i, j in up]
        last = lax.slice_in_dim(x, length - width, length, axis=dim)
        leading = lax.slice_in_dim(x, 0, width, axis=dim)
        before = lax.ppermute(last, axis, up)
        after = lax.ppermute(leading, axis, down)
        x = jnp.concatenate([before, x, after], axis=dim)
    return x


def local_kernel(factor, own_ref, fut_ref, up_ref, down_ref, fwd_ref, k_ref, feat_ref, gf_ref, term_ref, z_ref, a_ref):
    frames, breadth, channels = feat_ref.shape

    def slab(frame, row):
        if frame < frames:
            return (up_ref, own_ref, down_ref)[row][frame]
        if row == 1:
            return fut_ref[frame - frames]
        return fwd_ref[row // 2, frame - frames]

    lanes = lax.broadcasted_iota(jnp.int32, (channels, breadth), 1)
    for t in range(frames):
        values = feat_ref[t].astype(jnp.float32)
        active = (values * jax.nn.sigmoid(values)).astype(jnp.bfloat16).astype(jnp.float32)
        turned = active.T
        a_ref[t, 0:channels] = jnp.where(lanes == 0, 0.0, pltpu.roll(turned, 1, 1)).astype(a_ref.dtype)
        a_ref[t, channels : 2 * channels] = turned.astype(a_ref.dtype)
        a_ref[t, 2 * channels : 3 * channels] = jnp.where(
            lanes == breadth - 1, 0.0, pltpu.roll(turned, breadth - 1, 1)
        ).astype(a_ref.dtype)
    term_ref[...] = jnp.zeros_like(term_ref)
    rows = lax.broadcasted_iota(jnp.int32, (breadth, channels), 0)
    for t in range(frames):
        for i in range(3):
            for j in range(3):
                piece = slab(t + 2 - i, 2 - j)
                for k in range(3):
                    part = lax.dot_general(
                        piece,
                        k_ref[(i * 3 + j) * 3 + k],
                        (((1,), (1,)), ((), ())),
                        preferred_element_type=jnp.float32,
                    )
                    window = slice(k * channels, (k + 1) * channels)
                    if i == 0 and j == 0:
                        z_ref[:, window] = part
                    else:
                        z_ref[:, window] += part
                term_ref[i * 3 + j] += jnp.dot(a_ref[t], piece, preferred_element_type=jnp.float32)
        ahead = pltpu.roll(z_ref[:, 0:channels], breadth - 1, 0)
        behind = pltpu.roll(z_ref[:, 2 * channels : 3 * channels], 1, 0)
        grad_input = (
            jnp.where(rows == breadth - 1, 0.0, ahead)
            + z_ref[:, channels : 2 * channels]
            + jnp.where(rows == 0, 0.0, behind)
        )
        values = feat_ref[t].astype(jnp.float32)
        sigmoid_part = jax.nn.sigmoid(values)
        derivative = sigmoid_part * (1.0 + values * (1.0 - sigmoid_part))
        gf_ref[t] = (own_ref[t].astype(jnp.float32) + derivative * grad_input).astype(gf_ref.dtype)
    term_ref[...] = term_ref[...] * factor


def local_grads(pieces, weights, feat, factor):
    frames, breadth, channels = feat.shape
    vmem = pl.BlockSpec(memory_space=pltpu.VMEM)
    operands = tuple(pieces) + (weights, feat)
    flops = 2 * 2 * frames * 9 * breadth * channels * 3 * channels
    moved = sum(2 * x.size for x in operands) + 2 * feat.size + 4 * 9 * 3 * channels * channels
    return pl.pallas_call(
        lambda *refs: local_kernel(factor, *refs),
        out_shape=(
            jax.ShapeDtypeStruct((frames, breadth, channels), jnp.bfloat16),
            jax.ShapeDtypeStruct((9, 3 * channels, channels), jnp.float32),
        ),
        in_specs=[vmem] * len(operands),
        out_specs=(vmem, vmem),
        scratch_shapes=[
            pltpu.VMEM((breadth, 3 * channels), jnp.float32),
            pltpu.VMEM((frames, 3 * channels, breadth), jnp.bfloat16),
        ],
        compiler_params=pltpu.CompilerParams(vmem_limit_bytes=48 * 1024 * 1024),
        cost_estimate=pl.CostEstimate(flops=flops, bytes_accessed=moved, transcendentals=2 * feat.size),
    )(*operands)


def row_neighbours(x, axis):
    count = lax.axis_size(axis)
    up = [(i, i + 1) for i in range(count - 1)]
    down = [(j, i) for i, j in up]
    return lax.ppermute(x, axis, up), lax.ppermute(x, axis, down)


def body(features, cotangent, kernel):
    frames, height, breadth, channels = features.shape
    own = cotangent[:, 0]
    future = passed_along(own[:2], "ta", -1)
    above, below = row_neighbours(own, "ha")
    forwarded = passed_along(jnp.stack([above[:2], below[:2]]), "ta", -1)
    total_cells = frames * height * breadth * lax.axis_size("ha") * lax.axis_size("ta")
    factor = float(total_cells) ** (-0.5)
    weights = kernel.reshape(-1, channels, channels)
    grad_features, term = local_grads((own, future, above, below, forwarded), weights, features[:, 0], factor)
    term = term.reshape(-1, channels)
    owners = lax.axis_size("ha") * lax.axis_size("ta")
    rows = term.shape[0] // owners
    padded = -(-rows // 8) * 8
    term = jnp.pad(term.reshape(owners, rows, channels), ((0, 0), (0, padded - rows), (0, 0)))
    return (grad_features[:, None], term[None])


def physical_mesh(mesh):
    devices = mesh.devices
    coords = np.array([d.coords for d in devices.reshape(-1)])
    sizes = {"x": len(set(coords[:, 0])), "y": len(set(coords[:, 1])), "z": len(set(coords[:, 2]))}
    shape = tuple(sizes[a] for a in PHYSICAL) + (devices.shape[1],)
    grid = devices.reshape(shape)
    flat = np.array([d.coords for d in grid.reshape(-1)]).reshape(shape + (3,))
    want = np.stack(np.meshgrid(*[np.arange(n) for n in shape[:3]], indexing="ij"), -1)
    got = flat[..., 0, :][..., [1, 2, 0]]
    assert (got == want).all()
    return Mesh(grid, PHYSICAL + ("core",))


def reduce_blocks(term, order):
    rows = term.shape[2]
    part = term[0]
    for axis in order:
        count = lax.axis_size(axis)
        shaped = part.reshape((count, part.shape[0] // count) + part.shape[1:])
        part = lax.all_to_all(shaped, axis, 0, 0, tiled=True).sum(0)
    return part[0]


def solution(mesh):
    placed = (P("ta", "ha", None, None), P("ta", "ha", None, None), P())
    local = jax.shard_map(
        body,
        mesh=mesh,
        in_specs=placed,
        out_specs=(P("ta", "ha", None, None), P(("ha", "ta"))),
        check_vma=False,
    )
    grid = physical_mesh(mesh)
    order = ("core", "y", "z", "x")
    stages = ("core", PHYSICAL)
    names = PHYSICAL + ("core",)
    sizes = [grid.shape[a] for a in names]

    def reorder(term):
        n, owners, padded, channels = term.shape
        t = term.reshape((n,) + tuple(sizes) + (padded, channels))
        perm = [0] + [1 + names.index(a) for a in order] + [5, 6]
        return t.transpose(perm).reshape(n, owners, padded, channels)

    def reduce_fn(term):
        rows = 27
        return reduce_blocks(term, order)

    rows_per = None

    def run(features, cotangent, kernel):
        grad_features, term = local(features, cotangent, kernel)
        channels = kernel.shape[-1]
        owners = term.shape[1]
        taps_rows = kernel.shape[0] * kernel.shape[1] * kernel.shape[2] * kernel.shape[3]
        rows = taps_rows // owners
        term = reorder(term)
        spec = P(names)
        part = jax.shard_map(
            lambda t: reduce_blocks(t, stages)[:rows],
            mesh=grid,
            in_specs=spec,
            out_specs=P(names),
            check_vma=False,
        )(term)
        part = lax.with_sharding_constraint(part, NamedSharding(mesh, P(("ha", "ta"), None)))
        return grad_features, part

    return run
```

```python
import jax
import jax.numpy as jnp
import numpy as np
from jax import lax
from jax.sharding import Mesh, NamedSharding
from jax.sharding import PartitionSpec as P
from jax.experimental import pallas as pl
from jax.experimental.pallas import tpu as pltpu

PHYSICAL = ("y", "z", "x")


def passed_along(block, axis, distance):
    devices = range(lax.axis_size(axis))
    route = [(i - distance, i) for i in devices if i - distance in devices]
    return lax.ppermute(block, axis, route)


def with_halo(x, sides, width):
    for axis, dim in sides:
        count, length = (lax.axis_size(axis), x.shape[dim])
        up = [(i, (i + 1) % count) for i in range(count - 1)]
        down = [(j, i) for i, j in up]
        last = lax.slice_in_dim(x, length - width, length, axis=dim)
        leading = lax.slice_in_dim(x, 0, width, axis=dim)
        before = lax.ppermute(last, axis, up)
        after = lax.ppermute(leading, axis, down)
        x = jnp.concatenate([before, x, after], axis=dim)
    return x


def local_kernel(factor, own_ref, up_ref, down_ref, bnd_ref, k_ref, feat_ref, gf_ref, term_ref, z_ref, a_ref):
    frames, breadth, channels = feat_ref.shape

    def slab(frame, row):
        if frame < frames:
            return (up_ref, own_ref, down_ref)[row][frame]
        return bnd_ref[row, frame - frames]

    lanes = lax.broadcasted_iota(jnp.int32, (channels, breadth), 1)
    for t in range(frames):
        values = feat_ref[t].astype(jnp.float32)
        active = (values * jax.nn.sigmoid(values)).astype(jnp.bfloat16).astype(jnp.float32)
        turned = active.T
        a_ref[t, 0:channels] = jnp.where(lanes == 0, 0.0, pltpu.roll(turned, 1, 1)).astype(a_ref.dtype)
        a_ref[t, channels : 2 * channels] = turned.astype(a_ref.dtype)
        a_ref[t, 2 * channels : 3 * channels] = jnp.where(
            lanes == breadth - 1, 0.0, pltpu.roll(turned, breadth - 1, 1)
        ).astype(a_ref.dtype)
    term_ref[...] = jnp.zeros_like(term_ref)
    rows = lax.broadcasted_iota(jnp.int32, (breadth, channels), 0)
    for t in range(frames):
        for i in range(3):
            for j in range(3):
                piece = slab(t + 2 - i, 2 - j)
                for k in range(3):
                    part = lax.dot_general(
                        piece,
                        k_ref[(i * 3 + j) * 3 + k],
                        (((1,), (1,)), ((), ())),
                        preferred_element_type=jnp.float32,
                    )
                    window = slice(k * channels, (k + 1) * channels)
                    if i == 0 and j == 0:
                        z_ref[:, window] = part
                    else:
                        z_ref[:, window] += part
                term_ref[i * 3 + j] += jnp.dot(a_ref[t], piece, preferred_element_type=jnp.float32)
        ahead = pltpu.roll(z_ref[:, 0:channels], breadth - 1, 0)
        behind = pltpu.roll(z_ref[:, 2 * channels : 3 * channels], 1, 0)
        grad_input = (
            jnp.where(rows == breadth - 1, 0.0, ahead)
            + z_ref[:, channels : 2 * channels]
            + jnp.where(rows == 0, 0.0, behind)
        )
        values = feat_ref[t].astype(jnp.float32)
        sigmoid_part = jax.nn.sigmoid(values)
        derivative = sigmoid_part * (1.0 + values * (1.0 - sigmoid_part))
        gf_ref[t] = (own_ref[t].astype(jnp.float32) + derivative * grad_input).astype(gf_ref.dtype)
    term_ref[...] = term_ref[...] * factor


def local_grads(pieces, weights, feat, factor):
    frames, breadth, channels = feat.shape
    vmem = pl.BlockSpec(memory_space=pltpu.VMEM)
    operands = tuple(pieces) + (weights, feat)
    flops = 2 * 2 * frames * 9 * breadth * channels * 3 * channels
    moved = sum(2 * x.size for x in operands) + 2 * feat.size + 4 * 9 * 3 * channels * channels
    return pl.pallas_call(
        lambda *refs: local_kernel(factor, *refs),
        out_shape=(
            jax.ShapeDtypeStruct((frames, breadth, channels), jnp.bfloat16),
            jax.ShapeDtypeStruct((9, 3 * channels, channels), jnp.float32),
        ),
        in_specs=[vmem] * len(operands),
        out_specs=(vmem, vmem),
        scratch_shapes=[
            pltpu.VMEM((breadth, 3 * channels), jnp.float32),
            pltpu.VMEM((frames, 3 * channels, breadth), jnp.bfloat16),
        ],
        compiler_params=pltpu.CompilerParams(vmem_limit_bytes=48 * 1024 * 1024),
        cost_estimate=pl.CostEstimate(flops=flops, bytes_accessed=moved, transcendentals=2 * feat.size),
    )(*operands)


def row_neighbours(x, axis):
    count = lax.axis_size(axis)
    up = [(i, i + 1) for i in range(count - 1)]
    down = [(j, i) for i, j in up]
    return lax.ppermute(x, axis, up), lax.ppermute(x, axis, down)


def body(features, cotangent, kernel):
    frames, height, breadth, channels = features.shape
    own = cotangent[:, 0]
    above, below = row_neighbours(own, "ha")
    boundary = passed_along(jnp.stack([above[:2], own[:2], below[:2]]), "ta", -1)
    total_cells = frames * height * breadth * lax.axis_size("ha") * lax.axis_size("ta")
    factor = float(total_cells) ** (-0.5)
    weights = kernel.reshape(-1, channels, channels)
    grad_features, term = local_grads((own, above, below, boundary), weights, features[:, 0], factor)
    term = term.reshape(-1, channels)
    owners = lax.axis_size("ha") * lax.axis_size("ta")
    rows = term.shape[0] // owners
    padded = -(-rows // 8) * 8
    term = jnp.pad(term.reshape(owners, rows, channels), ((0, 0), (0, padded - rows), (0, 0)))
    return (grad_features[:, None], term[None])


def physical_mesh(mesh):
    devices = mesh.devices
    coords = np.array([d.coords for d in devices.reshape(-1)])
    sizes = {"x": len(set(coords[:, 0])), "y": len(set(coords[:, 1])), "z": len(set(coords[:, 2]))}
    shape = tuple(sizes[a] for a in PHYSICAL) + (devices.shape[1],)
    grid = devices.reshape(shape)
    flat = np.array([d.coords for d in grid.reshape(-1)]).reshape(shape + (3,))
    want = np.stack(np.meshgrid(*[np.arange(n) for n in shape[:3]], indexing="ij"), -1)
    got = flat[..., 0, :][..., [1, 2, 0]]
    assert (got == want).all()
    return Mesh(grid, PHYSICAL + ("core",))


def reduce_blocks(term, order):
    rows = term.shape[2]
    part = term[0]
    for axis in order:
        count = lax.axis_size(axis)
        shaped = part.reshape((count, part.shape[0] // count) + part.shape[1:])
        part = lax.all_to_all(shaped, axis, 0, 0, tiled=True).sum(0)
    return part[0]


def solution(mesh):
    placed = (P("ta", "ha", None, None), P("ta", "ha", None, None), P())
    local = jax.shard_map(
        body,
        mesh=mesh,
        in_specs=placed,
        out_specs=(P("ta", "ha", None, None), P(("ha", "ta"))),
        check_vma=False,
    )
    grid = physical_mesh(mesh)
    order = ("core", "y", "z", "x")
    stages = ("core", PHYSICAL)
    names = PHYSICAL + ("core",)
    sizes = [grid.shape[a] for a in names]

    def reorder(term):
        n, owners, padded, channels = term.shape
        t = term.reshape((n,) + tuple(sizes) + (padded, channels))
        perm = [0] + [1 + names.index(a) for a in order] + [5, 6]
        return t.transpose(perm).reshape(n, owners, padded, channels)

    def reduce_fn(term):
        rows = 27
        return reduce_blocks(term, order)

    rows_per = None

    def run(features, cotangent, kernel):
        grad_features, term = local(features, cotangent, kernel)
        channels = kernel.shape[-1]
        owners = term.shape[1]
        taps_rows = kernel.shape[0] * kernel.shape[1] * kernel.shape[2] * kernel.shape[3]
        rows = taps_rows // owners
        term = reorder(term)
        spec = P(names)
        part = jax.shard_map(
            lambda t: reduce_blocks(t, stages)[:rows],
            mesh=grid,
            in_specs=spec,
            out_specs=P(names),
            check_vma=False,
        )(term)
        part = lax.with_sharding_constraint(part, NamedSharding(mesh, P(("ha", "ta"), None)))
        return grad_features, part

    return run
```

```python
import jax
import jax.numpy as jnp
import numpy as np
from jax import lax
from jax.sharding import Mesh, NamedSharding
from jax.sharding import PartitionSpec as P
from jax.experimental import pallas as pl
from jax.experimental.pallas import tpu as pltpu

PHYSICAL = ("y", "z", "x")


def passed_along(block, axis, distance):
    devices = range(lax.axis_size(axis))
    route = [(i - distance, i) for i in devices if i - distance in devices]
    return lax.ppermute(block, axis, route)


def with_halo(x, sides, width):
    for axis, dim in sides:
        count, length = (lax.axis_size(axis), x.shape[dim])
        up = [(i, (i + 1) % count) for i in range(count - 1)]
        down = [(j, i) for i, j in up]
        last = lax.slice_in_dim(x, length - width, length, axis=dim)
        leading = lax.slice_in_dim(x, 0, width, axis=dim)
        before = lax.ppermute(last, axis, up)
        after = lax.ppermute(leading, axis, down)
        x = jnp.concatenate([before, x, after], axis=dim)
    return x


def local_kernel(factor, own_ref, up_ref, down_ref, bnd_ref, k_ref, feat_ref, gf_ref, term_ref, z_ref, a_ref, w_ref, cat_ref, acc_ref):
    frames, breadth, channels = feat_ref.shape

    def slab(frame, row):
        if frame < frames:
            return (up_ref, own_ref, down_ref)[row][frame]
        return bnd_ref[row, frame - frames]

    def block(n):
        return slice(n * channels, (n + 1) * channels)

    for i in range(3):
        for j in range(3):
            for k in range(3):
                w_ref[j, block(k), block(i)] = k_ref[(i * 3 + j) * 3 + k]
    lanes = lax.broadcasted_iota(jnp.int32, (channels, breadth), 1)
    for t in range(frames):
        values = feat_ref[t].astype(jnp.float32)
        active = (values * jax.nn.sigmoid(values)).astype(jnp.bfloat16).astype(jnp.float32)
        turned = active.T
        a_ref[t, block(0)] = jnp.where(lanes == 0, 0.0, pltpu.roll(turned, 1, 1)).astype(a_ref.dtype)
        a_ref[t, block(1)] = turned.astype(a_ref.dtype)
        a_ref[t, block(2)] = jnp.where(
            lanes == breadth - 1, 0.0, pltpu.roll(turned, breadth - 1, 1)
        ).astype(a_ref.dtype)
    acc_ref[...] = jnp.zeros_like(acc_ref)
    rows = lax.broadcasted_iota(jnp.int32, (breadth, channels), 0)
    for t in range(frames):
        for j in range(3):
            for i in range(3):
                cat_ref[:, block(i)] = slab(t + 2 - i, 2 - j)
            joined = cat_ref[...]
            part = lax.dot_general(
                joined, w_ref[j], (((1,), (1,)), ((), ())), preferred_element_type=jnp.float32
            )
            if j == 0:
                z_ref[...] = part
            else:
                z_ref[...] += part
            acc_ref[j] += jnp.dot(a_ref[t], joined, preferred_element_type=jnp.float32)
        ahead = pltpu.roll(z_ref[:, block(0)], breadth - 1, 0)
        behind = pltpu.roll(z_ref[:, block(2)], 1, 0)
        grad_input = (
            jnp.where(rows == breadth - 1, 0.0, ahead)
            + z_ref[:, block(1)]
            + jnp.where(rows == 0, 0.0, behind)
        )
        values = feat_ref[t].astype(jnp.float32)
        sigmoid_part = jax.nn.sigmoid(values)
        derivative = sigmoid_part * (1.0 + values * (1.0 - sigmoid_part))
        gf_ref[t] = (own_ref[t].astype(jnp.float32) + derivative * grad_input).astype(gf_ref.dtype)
    for i in range(3):
        for j in range(3):
            term_ref[i * 3 + j] = acc_ref[j, :, block(i)] * factor


def local_grads(pieces, weights, feat, factor):
    frames, breadth, channels = feat.shape
    vmem = pl.BlockSpec(memory_space=pltpu.VMEM)
    operands = tuple(pieces) + (weights, feat)
    flops = 2 * 2 * frames * 9 * breadth * channels * 3 * channels
    moved = sum(2 * x.size for x in operands) + 2 * feat.size + 4 * 9 * 3 * channels * channels
    return pl.pallas_call(
        lambda *refs: local_kernel(factor, *refs),
        out_shape=(
            jax.ShapeDtypeStruct((frames, breadth, channels), jnp.bfloat16),
            jax.ShapeDtypeStruct((9, 3 * channels, channels), jnp.float32),
        ),
        in_specs=[vmem] * len(operands),
        out_specs=(vmem, vmem),
        scratch_shapes=[
            pltpu.VMEM((breadth, 3 * channels), jnp.float32),
            pltpu.VMEM((frames, 3 * channels, breadth), jnp.bfloat16),
            pltpu.VMEM((3, 3 * channels, 3 * channels), jnp.bfloat16),
            pltpu.VMEM((breadth, 3 * channels), jnp.bfloat16),
            pltpu.VMEM((3, 3 * channels, 3 * channels), jnp.float32),
        ],
        compiler_params=pltpu.CompilerParams(vmem_limit_bytes=48 * 1024 * 1024),
        cost_estimate=pl.CostEstimate(flops=flops, bytes_accessed=moved, transcendentals=2 * feat.size),
    )(*operands)


def row_neighbours(x, axis):
    count = lax.axis_size(axis)
    up = [(i, i + 1) for i in range(count - 1)]
    down = [(j, i) for i, j in up]
    return lax.ppermute(x, axis, up), lax.ppermute(x, axis, down)


def body(features, cotangent, kernel):
    frames, height, breadth, channels = features.shape
    own = cotangent[:, 0]
    above, below = row_neighbours(own, "ha")
    boundary = passed_along(jnp.stack([above[:2], own[:2], below[:2]]), "ta", -1)
    total_cells = frames * height * breadth * lax.axis_size("ha") * lax.axis_size("ta")
    factor = float(total_cells) ** (-0.5)
    weights = kernel.reshape(-1, channels, channels)
    grad_features, term = local_grads((own, above, below, boundary), weights, features[:, 0], factor)
    term = term.reshape(-1, channels)
    owners = lax.axis_size("ha") * lax.axis_size("ta")
    rows = term.shape[0] // owners
    padded = -(-rows // 8) * 8
    term = jnp.pad(term.reshape(owners, rows, channels), ((0, 0), (0, padded - rows), (0, 0)))
    return (grad_features[:, None], term[None])


def physical_mesh(mesh):
    devices = mesh.devices
    coords = np.array([d.coords for d in devices.reshape(-1)])
    sizes = {"x": len(set(coords[:, 0])), "y": len(set(coords[:, 1])), "z": len(set(coords[:, 2]))}
    shape = tuple(sizes[a] for a in PHYSICAL) + (devices.shape[1],)
    grid = devices.reshape(shape)
    flat = np.array([d.coords for d in grid.reshape(-1)]).reshape(shape + (3,))
    want = np.stack(np.meshgrid(*[np.arange(n) for n in shape[:3]], indexing="ij"), -1)
    got = flat[..., 0, :][..., [1, 2, 0]]
    assert (got == want).all()
    return Mesh(grid, PHYSICAL + ("core",))


def reduce_blocks(term, order):
    rows = term.shape[2]
    part = term[0]
    for axis in order:
        count = lax.axis_size(axis)
        shaped = part.reshape((count, part.shape[0] // count) + part.shape[1:])
        part = lax.all_to_all(shaped, axis, 0, 0, tiled=True).sum(0)
    return part[0]


def solution(mesh):
    placed = (P("ta", "ha", None, None), P("ta", "ha", None, None), P())
    local = jax.shard_map(
        body,
        mesh=mesh,
        in_specs=placed,
        out_specs=(P("ta", "ha", None, None), P(("ha", "ta"))),
        check_vma=False,
    )
    grid = physical_mesh(mesh)
    order = ("core", "y", "z", "x")
    stages = ("core", PHYSICAL)
    names = PHYSICAL + ("core",)
    sizes = [grid.shape[a] for a in names]

    def reorder(term):
        n, owners, padded, channels = term.shape
        t = term.reshape((n,) + tuple(sizes) + (padded, channels))
        perm = [0] + [1 + names.index(a) for a in order] + [5, 6]
        return t.transpose(perm).reshape(n, owners, padded, channels)

    def reduce_fn(term):
        rows = 27
        return reduce_blocks(term, order)

    rows_per = None

    def run(features, cotangent, kernel):
        grad_features, term = local(features, cotangent, kernel)
        channels = kernel.shape[-1]
        owners = term.shape[1]
        taps_rows = kernel.shape[0] * kernel.shape[1] * kernel.shape[2] * kernel.shape[3]
        rows = taps_rows // owners
        term = reorder(term)
        spec = P(names)
        part = jax.shard_map(
            lambda t: reduce_blocks(t, stages)[:rows],
            mesh=grid,
            in_specs=spec,
            out_specs=P(names),
            check_vma=False,
        )(term)
        part = lax.with_sharding_constraint(part, NamedSharding(mesh, P(("ha", "ta"), None)))
        return grad_features, part

    return run
```

```python
import jax
import jax.numpy as jnp
import numpy as np
from jax import lax
from jax.sharding import Mesh, NamedSharding
from jax.sharding import PartitionSpec as P
from jax.experimental import pallas as pl
from jax.experimental.pallas import tpu as pltpu

PHYSICAL = ("y", "z", "x")


def passed_along(block, axis, distance):
    devices = range(lax.axis_size(axis))
    route = [(i - distance, i) for i in devices if i - distance in devices]
    return lax.ppermute(block, axis, route)


def with_halo(x, sides, width):
    for axis, dim in sides:
        count, length = (lax.axis_size(axis), x.shape[dim])
        up = [(i, (i + 1) % count) for i in range(count - 1)]
        down = [(j, i) for i, j in up]
        last = lax.slice_in_dim(x, length - width, length, axis=dim)
        leading = lax.slice_in_dim(x, 0, width, axis=dim)
        before = lax.ppermute(last, axis, up)
        after = lax.ppermute(leading, axis, down)
        x = jnp.concatenate([before, x, after], axis=dim)
    return x


def slab_reader(own_ref, up_ref, down_ref, bnd_ref, frames):
    def slab(frame, row):
        if frame < frames:
            return (up_ref, own_ref, down_ref)[row][frame]
        return bnd_ref[row, frame - frames]

    return slab


def block(n, channels):
    return slice(n * channels, (n + 1) * channels)


def join_slabs(slab, cat_ref, t, j, channels):
    for i in range(3):
        cat_ref[:, block(i, channels)] = slab(t + 2 - i, 2 - j)
    return cat_ref[...]


def term_kernel(factor, own_ref, up_ref, down_ref, bnd_ref, feat_ref, term_ref, a_ref, cat_ref, acc_ref):
    frames, breadth, channels = feat_ref.shape
    slab = slab_reader(own_ref, up_ref, down_ref, bnd_ref, frames)
    lanes = lax.broadcasted_iota(jnp.int32, (channels, breadth), 1)
    for t in range(frames):
        values = feat_ref[t].astype(jnp.float32)
        active = (values * jax.nn.sigmoid(values)).astype(jnp.bfloat16).astype(jnp.float32)
        turned = active.T
        a_ref[t, block(0, channels)] = jnp.where(lanes == 0, 0.0, pltpu.roll(turned, 1, 1)).astype(a_ref.dtype)
        a_ref[t, block(1, channels)] = turned.astype(a_ref.dtype)
        a_ref[t, block(2, channels)] = jnp.where(
            lanes == breadth - 1, 0.0, pltpu.roll(turned, breadth - 1, 1)
        ).astype(a_ref.dtype)
    acc_ref[...] = jnp.zeros_like(acc_ref)
    for t in range(frames):
        for j in range(3):
            joined = join_slabs(slab, cat_ref, t, j, channels)
            acc_ref[j] += jnp.dot(a_ref[t], joined, preferred_element_type=jnp.float32)
    for i in range(3):
        for j in range(3):
            term_ref[i * 3 + j] = acc_ref[j, :, block(i, channels)] * factor


def grad_kernel(own_ref, up_ref, down_ref, bnd_ref, k_ref, feat_ref, gf_ref, z_ref, w_ref, cat_ref):
    frames, breadth, channels = feat_ref.shape
    slab = slab_reader(own_ref, up_ref, down_ref, bnd_ref, frames)
    for i in range(3):
        for j in range(3):
            for k in range(3):
                w_ref[j, block(k, channels), block(i, channels)] = k_ref[(i * 3 + j) * 3 + k]
    rows = lax.broadcasted_iota(jnp.int32, (breadth, channels), 0)
    for t in range(frames):
        for j in range(3):
            joined = join_slabs(slab, cat_ref, t, j, channels)
            part = lax.dot_general(
                joined, w_ref[j], (((1,), (1,)), ((), ())), preferred_element_type=jnp.float32
            )
            if j == 0:
                z_ref[...] = part
            else:
                z_ref[...] += part
        ahead = pltpu.roll(z_ref[:, block(0, channels)], breadth - 1, 0)
        behind = pltpu.roll(z_ref[:, block(2, channels)], 1, 0)
        grad_input = (
            jnp.where(rows == breadth - 1, 0.0, ahead)
            + z_ref[:, block(1, channels)]
            + jnp.where(rows == 0, 0.0, behind)
        )
        values = feat_ref[t].astype(jnp.float32)
        sigmoid_part = jax.nn.sigmoid(values)
        derivative = sigmoid_part * (1.0 + values * (1.0 - sigmoid_part))
        gf_ref[t] = (own_ref[t].astype(jnp.float32) + derivative * grad_input).astype(gf_ref.dtype)


def local_grads(pieces, weights, feat, factor):
    frames, breadth, channels = feat.shape
    vmem = pl.BlockSpec(memory_space=pltpu.VMEM)
    params = pltpu.CompilerParams(vmem_limit_bytes=48 * 1024 * 1024)
    flops = 2 * frames * 9 * breadth * channels * 3 * channels
    piece_bytes = sum(2 * x.size for x in pieces)
    term = pl.pallas_call(
        lambda *refs: term_kernel(factor, *refs),
        out_shape=jax.ShapeDtypeStruct((9, 3 * channels, channels), jnp.float32),
        in_specs=[vmem] * (len(pieces) + 1),
        out_specs=vmem,
        scratch_shapes=[
            pltpu.VMEM((frames, 3 * channels, breadth), jnp.bfloat16),
            pltpu.VMEM((breadth, 3 * channels), jnp.bfloat16),
            pltpu.VMEM((3, 3 * channels, 3 * channels), jnp.float32),
        ],
        compiler_params=params,
        cost_estimate=pl.CostEstimate(
            flops=flops, bytes_accessed=piece_bytes + 2 * feat.size + 4 * 27 * channels * channels,
            transcendentals=feat.size,
        ),
    )(*pieces, feat)
    grad_features = pl.pallas_call(
        grad_kernel,
        out_shape=jax.ShapeDtypeStruct((frames, breadth, channels), jnp.bfloat16),
        in_specs=[vmem] * (len(pieces) + 2),
        out_specs=vmem,
        scratch_shapes=[
            pltpu.VMEM((breadth, 3 * channels), jnp.float32),
            pltpu.VMEM((3, 3 * channels, 3 * channels), jnp.bfloat16),
            pltpu.VMEM((breadth, 3 * channels), jnp.bfloat16),
        ],
        compiler_params=params,
        cost_estimate=pl.CostEstimate(
            flops=flops, bytes_accessed=piece_bytes + 2 * weights.size + 4 * feat.size,
            transcendentals=feat.size,
        ),
    )(*pieces, weights, feat)
    return grad_features, term


def row_neighbours(x, axis):
    count = lax.axis_size(axis)
    up = [(i, i + 1) for i in range(count - 1)]
    down = [(j, i) for i, j in up]
    return lax.ppermute(x, axis, up), lax.ppermute(x, axis, down)


def body(features, cotangent, kernel):
    frames, height, breadth, channels = features.shape
    own = cotangent[:, 0]
    above, below = row_neighbours(own, "ha")
    boundary = passed_along(jnp.stack([above[:2], own[:2], below[:2]]), "ta", -1)
    total_cells = frames * height * breadth * lax.axis_size("ha") * lax.axis_size("ta")
    factor = float(total_cells) ** (-0.5)
    weights = kernel.reshape(-1, channels, channels)
    grad_features, term = local_grads((own, above, below, boundary), weights, features[:, 0], factor)
    term = term.reshape(-1, channels)
    owners = lax.axis_size("ha") * lax.axis_size("ta")
    rows = term.shape[0] // owners
    padded = -(-rows // 8) * 8
    term = jnp.pad(term.reshape(owners, rows, channels), ((0, 0), (0, padded - rows), (0, 0)))
    return (grad_features[:, None], term[None])


def physical_mesh(mesh):
    devices = mesh.devices
    coords = np.array([d.coords for d in devices.reshape(-1)])
    sizes = {"x": len(set(coords[:, 0])), "y": len(set(coords[:, 1])), "z": len(set(coords[:, 2]))}
    shape = tuple(sizes[a] for a in PHYSICAL) + (devices.shape[1],)
    grid = devices.reshape(shape)
    flat = np.array([d.coords for d in grid.reshape(-1)]).reshape(shape + (3,))
    want = np.stack(np.meshgrid(*[np.arange(n) for n in shape[:3]], indexing="ij"), -1)
    got = flat[..., 0, :][..., [1, 2, 0]]
    assert (got == want).all()
    return Mesh(grid, PHYSICAL + ("core",))


def reduce_blocks(term, order):
    rows = term.shape[2]
    part = term[0]
    for axis in order:
        count = lax.axis_size(axis)
        shaped = part.reshape((count, part.shape[0] // count) + part.shape[1:])
        part = lax.all_to_all(shaped, axis, 0, 0, tiled=True).sum(0)
    return part[0]


def solution(mesh):
    placed = (P("ta", "ha", None, None), P("ta", "ha", None, None), P())
    local = jax.shard_map(
        body,
        mesh=mesh,
        in_specs=placed,
        out_specs=(P("ta", "ha", None, None), P(("ha", "ta"))),
        check_vma=False,
    )
    grid = physical_mesh(mesh)
    order = ("core", "y", "z", "x")
    stages = ("core", PHYSICAL)
    names = PHYSICAL + ("core",)
    sizes = [grid.shape[a] for a in names]

    def reorder(term):
        n, owners, padded, channels = term.shape
        t = term.reshape((n,) + tuple(sizes) + (padded, channels))
        perm = [0] + [1 + names.index(a) for a in order] + [5, 6]
        return t.transpose(perm).reshape(n, owners, padded, channels)

    def reduce_fn(term):
        rows = 27
        return reduce_blocks(term, order)

    rows_per = None

    def run(features, cotangent, kernel):
        grad_features, term = local(features, cotangent, kernel)
        channels = kernel.shape[-1]
        owners = term.shape[1]
        taps_rows = kernel.shape[0] * kernel.shape[1] * kernel.shape[2] * kernel.shape[3]
        rows = taps_rows // owners
        term = reorder(term)
        spec = P(names)
        part = jax.shard_map(
            lambda t: reduce_blocks(t, stages)[:rows],
            mesh=grid,
            in_specs=spec,
            out_specs=P(names),
            check_vma=False,
        )(term)
        part = lax.with_sharding_constraint(part, NamedSharding(mesh, P(("ha", "ta"), None)))
        return grad_features, part

    return run
```

```python
import jax
import jax.numpy as jnp
import numpy as np
from jax import lax
from jax.sharding import Mesh, NamedSharding
from jax.sharding import PartitionSpec as P
from jax.experimental import pallas as pl
from jax.experimental.pallas import tpu as pltpu

PHYSICAL = ("y", "z", "x")


def passed_along(block, axis, distance):
    devices = range(lax.axis_size(axis))
    route = [(i - distance, i) for i in devices if i - distance in devices]
    return lax.ppermute(block, axis, route)


def with_halo(x, sides, width):
    for axis, dim in sides:
        count, length = (lax.axis_size(axis), x.shape[dim])
        up = [(i, (i + 1) % count) for i in range(count - 1)]
        down = [(j, i) for i, j in up]
        last = lax.slice_in_dim(x, length - width, length, axis=dim)
        leading = lax.slice_in_dim(x, 0, width, axis=dim)
        before = lax.ppermute(last, axis, up)
        after = lax.ppermute(leading, axis, down)
        x = jnp.concatenate([before, x, after], axis=dim)
    return x


def local_kernel(factor, own_ref, up_ref, down_ref, bnd_ref, k_ref, feat_ref, gf_ref, term_ref, z_ref, a_ref, w_ref, cat_ref, acc_ref):
    frames, breadth, channels = feat_ref.shape

    def slab(frame, row):
        if frame < frames:
            return (up_ref, own_ref, down_ref)[row][frame]
        return bnd_ref[row, frame - frames]

    def block(n):
        return slice(n * channels, (n + 1) * channels)

    for i in range(3):
        for j in range(3):
            for k in range(3):
                w_ref[j, block(k), block(i)] = k_ref[(i * 3 + j) * 3 + k]
    lanes = lax.broadcasted_iota(jnp.int32, (channels, breadth), 1)
    for t in range(frames):
        values = feat_ref[t].astype(jnp.float32)
        active = (values * jax.nn.sigmoid(values)).astype(jnp.bfloat16).astype(jnp.float32)
        turned = active.T
        a_ref[t, block(0)] = jnp.where(lanes == 0, 0.0, pltpu.roll(turned, 1, 1)).astype(a_ref.dtype)
        a_ref[t, block(1)] = turned.astype(a_ref.dtype)
        a_ref[t, block(2)] = jnp.where(
            lanes == breadth - 1, 0.0, pltpu.roll(turned, breadth - 1, 1)
        ).astype(a_ref.dtype)
    acc_ref[...] = jnp.zeros_like(acc_ref)
    rows = lax.broadcasted_iota(jnp.int32, (breadth, channels), 0)
    for t in range(frames):
        for j in range(3):
            for i in range(3):
                cat_ref[:, block(i)] = slab(t + 2 - i, 2 - j)
            joined = cat_ref[...]
            part = lax.dot_general(
                joined, w_ref[j], (((1,), (1,)), ((), ())), preferred_element_type=jnp.float32
            )
            if j == 0:
                z_ref[...] = part
            else:
                z_ref[...] += part
            acc_ref[j] += jnp.dot(a_ref[t], joined, preferred_element_type=jnp.float32)
        ahead = pltpu.roll(z_ref[:, block(0)], breadth - 1, 0)
        behind = pltpu.roll(z_ref[:, block(2)], 1, 0)
        grad_input = (
            jnp.where(rows == breadth - 1, 0.0, ahead)
            + z_ref[:, block(1)]
            + jnp.where(rows == 0, 0.0, behind)
        )
        values = feat_ref[t].astype(jnp.float32)
        sigmoid_part = jax.nn.sigmoid(values)
        derivative = sigmoid_part * (1.0 + values * (1.0 - sigmoid_part))
        gf_ref[t] = (own_ref[t].astype(jnp.float32) + derivative * grad_input).astype(gf_ref.dtype)
    for i in range(3):
        for j in range(3):
            term_ref[i * 3 + j] = acc_ref[j, :, block(i)] * factor


def local_grads(pieces, weights, feat, factor):
    frames, breadth, channels = feat.shape
    vmem = pl.BlockSpec(memory_space=pltpu.VMEM)
    operands = tuple(pieces) + (weights, feat)
    flops = 2 * 2 * frames * 9 * breadth * channels * 3 * channels
    moved = sum(2 * x.size for x in operands) + 2 * feat.size + 4 * 9 * 3 * channels * channels
    return pl.pallas_call(
        lambda *refs: local_kernel(factor, *refs),
        out_shape=(
            jax.ShapeDtypeStruct((frames, breadth, channels), jnp.bfloat16),
            jax.ShapeDtypeStruct((9, 3 * channels, channels), jnp.float32),
        ),
        in_specs=[vmem] * len(operands),
        out_specs=(vmem, vmem),
        scratch_shapes=[
            pltpu.VMEM((breadth, 3 * channels), jnp.float32),
            pltpu.VMEM((frames, 3 * channels, breadth), jnp.bfloat16),
            pltpu.VMEM((3, 3 * channels, 3 * channels), jnp.bfloat16),
            pltpu.VMEM((breadth, 3 * channels), jnp.bfloat16),
            pltpu.VMEM((3, 3 * channels, 3 * channels), jnp.float32),
        ],
        compiler_params=pltpu.CompilerParams(vmem_limit_bytes=48 * 1024 * 1024),
        cost_estimate=pl.CostEstimate(flops=flops, bytes_accessed=moved, transcendentals=2 * feat.size),
    )(*operands)


def row_neighbours(x, axis):
    count = lax.axis_size(axis)
    up = [(i, i + 1) for i in range(count - 1)]
    down = [(j, i) for i, j in up]
    return lax.ppermute(x, axis, up), lax.ppermute(x, axis, down)


def body(features, cotangent, kernel):
    frames, height, breadth, channels = features.shape
    own = cotangent[:, 0]
    above, below = row_neighbours(own, "ha")
    boundary = passed_along(jnp.stack([above[:2], own[:2], below[:2]]), "ta", -1)
    total_cells = frames * height * breadth * lax.axis_size("ha") * lax.axis_size("ta")
    factor = float(total_cells) ** (-0.5)
    weights = kernel.reshape(-1, channels, channels)
    grad_features, term = local_grads((own, above, below, boundary), weights, features[:, 0], factor)
    term = term.reshape(-1, channels)
    owners = lax.axis_size("ha") * lax.axis_size("ta")
    rows = term.shape[0] // owners
    padded = -(-rows // 8) * 8
    term = jnp.pad(term.reshape(owners, rows, channels), ((0, 0), (0, padded - rows), (0, 0)))
    return (grad_features[:, None], term[None])


def physical_mesh(mesh):
    devices = mesh.devices
    coords = np.array([d.coords for d in devices.reshape(-1)])
    sizes = {"x": len(set(coords[:, 0])), "y": len(set(coords[:, 1])), "z": len(set(coords[:, 2]))}
    shape = tuple(sizes[a] for a in PHYSICAL) + (devices.shape[1],)
    grid = devices.reshape(shape)
    flat = np.array([d.coords for d in grid.reshape(-1)]).reshape(shape + (3,))
    want = np.stack(np.meshgrid(*[np.arange(n) for n in shape[:3]], indexing="ij"), -1)
    got = flat[..., 0, :][..., [1, 2, 0]]
    assert (got == want).all()
    return Mesh(grid, PHYSICAL + ("core",))


def reduce_blocks(term, order):
    rows = term.shape[2]
    part = term[0]
    for axis in order:
        count = lax.axis_size(axis)
        shaped = part.reshape((count, part.shape[0] // count) + part.shape[1:])
        if count == 2 and not isinstance(axis, tuple):
            first = lax.axis_index(axis) == 0
            kept = jnp.where(first, shaped[0], shaped[1])
            sent = jnp.where(first, shaped[1], shaped[0])
            part = kept + lax.ppermute(sent, axis, [(0, 1), (1, 0)])
        else:
            part = lax.all_to_all(shaped, axis, 0, 0, tiled=True).sum(0)
    return part[0]


def solution(mesh):
    placed = (P("ta", "ha", None, None), P("ta", "ha", None, None), P())
    local = jax.shard_map(
        body,
        mesh=mesh,
        in_specs=placed,
        out_specs=(P("ta", "ha", None, None), P(("ha", "ta"))),
        check_vma=False,
    )
    grid = physical_mesh(mesh)
    order = ("core", "y", "z", "x")
    stages = ("core", PHYSICAL)
    names = PHYSICAL + ("core",)
    sizes = [grid.shape[a] for a in names]

    def reorder(term):
        n, owners, padded, channels = term.shape
        t = term.reshape((n,) + tuple(sizes) + (padded, channels))
        perm = [0] + [1 + names.index(a) for a in order] + [5, 6]
        return t.transpose(perm).reshape(n, owners, padded, channels)

    def reduce_fn(term):
        rows = 27
        return reduce_blocks(term, order)

    rows_per = None

    def run(features, cotangent, kernel):
        grad_features, term = local(features, cotangent, kernel)
        channels = kernel.shape[-1]
        owners = term.shape[1]
        taps_rows = kernel.shape[0] * kernel.shape[1] * kernel.shape[2] * kernel.shape[3]
        rows = taps_rows // owners
        term = reorder(term)
        spec = P(names)
        part = jax.shard_map(
            lambda t: reduce_blocks(t, stages)[:rows],
            mesh=grid,
            in_specs=spec,
            out_specs=P(names),
            check_vma=False,
        )(term)
        part = lax.with_sharding_constraint(part, NamedSharding(mesh, P(("ha", "ta"), None)))
        return grad_features, part

    return run
```

```python
import jax
import jax.numpy as jnp
import numpy as np
from jax import lax
from jax.sharding import Mesh, NamedSharding
from jax.sharding import PartitionSpec as P
from jax.experimental import pallas as pl
from jax.experimental.pallas import tpu as pltpu

PHYSICAL = ("y", "z", "x")


def passed_along(block, axis, distance):
    devices = range(lax.axis_size(axis))
    route = [(i - distance, i) for i in devices if i - distance in devices]
    return lax.ppermute(block, axis, route)


def with_halo(x, sides, width):
    for axis, dim in sides:
        count, length = (lax.axis_size(axis), x.shape[dim])
        up = [(i, (i + 1) % count) for i in range(count - 1)]
        down = [(j, i) for i, j in up]
        last = lax.slice_in_dim(x, length - width, length, axis=dim)
        leading = lax.slice_in_dim(x, 0, width, axis=dim)
        before = lax.ppermute(last, axis, up)
        after = lax.ppermute(leading, axis, down)
        x = jnp.concatenate([before, x, after], axis=dim)
    return x


def local_kernel(factor, own_ref, up_ref, down_ref, bnd_ref, k_ref, feat_ref, gf_ref, term_ref, z_ref, a_ref, w_ref, cat_ref, acc_ref):
    frames, breadth, channels = feat_ref.shape

    def slab(frame, row):
        if frame < frames:
            return (up_ref, own_ref, down_ref)[row][frame]
        return bnd_ref[row, frame - frames]

    def block(n):
        return slice(n * channels, (n + 1) * channels)

    for i in range(3):
        for j in range(3):
            for k in range(3):
                w_ref[j, block(k), block(i)] = k_ref[(i * 3 + j) * 3 + k]
    lanes = lax.broadcasted_iota(jnp.int32, (channels, breadth), 1)
    for t in range(frames):
        values = feat_ref[t].astype(jnp.float32)
        active = (values * jax.nn.sigmoid(values)).astype(jnp.bfloat16).astype(jnp.float32)
        turned = active.T
        a_ref[t, block(0)] = jnp.where(lanes == 0, 0.0, pltpu.roll(turned, 1, 1)).astype(a_ref.dtype)
        a_ref[t, block(1)] = turned.astype(a_ref.dtype)
        a_ref[t, block(2)] = jnp.where(
            lanes == breadth - 1, 0.0, pltpu.roll(turned, breadth - 1, 1)
        ).astype(a_ref.dtype)
    acc_ref[...] = jnp.zeros_like(acc_ref)
    rows = lax.broadcasted_iota(jnp.int32, (breadth, channels), 0)
    for t in range(frames):
        for j in range(3):
            for i in range(3):
                cat_ref[:, block(i)] = slab(t + 2 - i, 2 - j)
            joined = cat_ref[...]
            part = lax.dot_general(
                joined, w_ref[j], (((1,), (1,)), ((), ())), preferred_element_type=jnp.float32
            )
            if j == 0:
                z_ref[...] = part
            else:
                z_ref[...] += part
            acc_ref[j] += jnp.dot(a_ref[t], joined, preferred_element_type=jnp.float32)
        ahead = pltpu.roll(z_ref[:, block(0)], breadth - 1, 0)
        behind = pltpu.roll(z_ref[:, block(2)], 1, 0)
        grad_input = (
            jnp.where(rows == breadth - 1, 0.0, ahead)
            + z_ref[:, block(1)]
            + jnp.where(rows == 0, 0.0, behind)
        )
        values = feat_ref[t].astype(jnp.float32)
        sigmoid_part = jax.nn.sigmoid(values)
        derivative = sigmoid_part * (1.0 + values * (1.0 - sigmoid_part))
        gf_ref[t] = (own_ref[t].astype(jnp.float32) + derivative * grad_input).astype(gf_ref.dtype)
    for i in range(3):
        for j in range(3):
            term_ref[i * 3 + j] = acc_ref[j, :, block(i)] * factor


def local_grads(pieces, weights, feat, factor):
    frames, breadth, channels = feat.shape
    vmem = pl.BlockSpec(memory_space=pltpu.VMEM)
    operands = tuple(pieces) + (weights, feat)
    flops = 2 * 2 * frames * 9 * breadth * channels * 3 * channels
    moved = sum(2 * x.size for x in operands) + 2 * feat.size + 4 * 9 * 3 * channels * channels
    return pl.pallas_call(
        lambda *refs: local_kernel(factor, *refs),
        out_shape=(
            jax.ShapeDtypeStruct((frames, breadth, channels), jnp.bfloat16),
            jax.ShapeDtypeStruct((9, 3 * channels, channels), jnp.float32),
        ),
        in_specs=[vmem] * len(operands),
        out_specs=(vmem, vmem),
        scratch_shapes=[
            pltpu.VMEM((breadth, 3 * channels), jnp.float32),
            pltpu.VMEM((frames, 3 * channels, breadth), jnp.bfloat16),
            pltpu.VMEM((3, 3 * channels, 3 * channels), jnp.bfloat16),
            pltpu.VMEM((breadth, 3 * channels), jnp.bfloat16),
            pltpu.VMEM((3, 3 * channels, 3 * channels), jnp.float32),
        ],
        compiler_params=pltpu.CompilerParams(vmem_limit_bytes=48 * 1024 * 1024),
        cost_estimate=pl.CostEstimate(flops=flops, bytes_accessed=moved, transcendentals=2 * feat.size),
    )(*operands)


def row_neighbours(x, axis):
    count = lax.axis_size(axis)
    up = [(i, i + 1) for i in range(count - 1)]
    down = [(j, i) for i, j in up]
    return lax.ppermute(x, axis, up), lax.ppermute(x, axis, down)


def body(features, cotangent, kernel):
    frames, height, breadth, channels = features.shape
    own = cotangent[:, 0]
    above, below = row_neighbours(own, "ha")
    boundary = passed_along(jnp.stack([above[:2], own[:2], below[:2]]), "ta", -1)
    total_cells = frames * height * breadth * lax.axis_size("ha") * lax.axis_size("ta")
    factor = float(total_cells) ** (-0.5)
    weights = kernel.reshape(-1, channels, channels)
    grad_features, term = local_grads((own, above, below, boundary), weights, features[:, 0], factor)
    term = term.reshape(-1, channels)
    owners = lax.axis_size("ha") * lax.axis_size("ta")
    rows = term.shape[0] // owners
    padded = -(-rows // 8) * 8
    term = jnp.pad(term.reshape(owners, rows, channels), ((0, 0), (0, padded - rows), (0, 0)))
    total = lax.all_to_all(term, ("ha", "ta"), 0, 0, tiled=True).sum(0)
    return (grad_features[:, None], total[:rows])


def physical_mesh(mesh):
    devices = mesh.devices
    coords = np.array([d.coords for d in devices.reshape(-1)])
    sizes = {"x": len(set(coords[:, 0])), "y": len(set(coords[:, 1])), "z": len(set(coords[:, 2]))}
    shape = tuple(sizes[a] for a in PHYSICAL) + (devices.shape[1],)
    grid = devices.reshape(shape)
    flat = np.array([d.coords for d in grid.reshape(-1)]).reshape(shape + (3,))
    want = np.stack(np.meshgrid(*[np.arange(n) for n in shape[:3]], indexing="ij"), -1)
    got = flat[..., 0, :][..., [1, 2, 0]]
    assert (got == want).all()
    return Mesh(grid, PHYSICAL + ("core",))


def reduce_blocks(term, order):
    rows = term.shape[2]
    part = term[0]
    for axis in order:
        count = lax.axis_size(axis)
        shaped = part.reshape((count, part.shape[0] // count) + part.shape[1:])
        part = lax.all_to_all(shaped, axis, 0, 0, tiled=True).sum(0)
    return part[0]


def solution(mesh):
    placed = (P("ta", "ha", None, None), P("ta", "ha", None, None), P())
    return jax.shard_map(
        body,
        mesh=mesh,
        in_specs=placed,
        out_specs=(P("ta", "ha", None, None), P(("ha", "ta"), None)),
        check_vma=False,
    )
```

```python
import jax
import jax.numpy as jnp
import numpy as np
from jax import lax
from jax.sharding import Mesh, NamedSharding
from jax.sharding import PartitionSpec as P
from jax.experimental import pallas as pl
from jax.experimental.pallas import tpu as pltpu

PHYSICAL = ("y", "z", "x")


def passed_along(block, axis, distance):
    devices = range(lax.axis_size(axis))
    route = [(i - distance, i) for i in devices if i - distance in devices]
    return lax.ppermute(block, axis, route)


def with_halo(x, sides, width):
    for axis, dim in sides:
        count, length = (lax.axis_size(axis), x.shape[dim])
        up = [(i, (i + 1) % count) for i in range(count - 1)]
        down = [(j, i) for i, j in up]
        last = lax.slice_in_dim(x, length - width, length, axis=dim)
        leading = lax.slice_in_dim(x, 0, width, axis=dim)
        before = lax.ppermute(last, axis, up)
        after = lax.ppermute(leading, axis, down)
        x = jnp.concatenate([before, x, after], axis=dim)
    return x


def local_kernel(factor, own_ref, up_ref, down_ref, bnd_ref, k_hbm, feat_hbm, gf_ref, term_ref, z_ref, a_ref, w_ref, cat_ref, acc_ref, k_ref, feat_ref, sems):
    frames, breadth, channels = feat_ref.shape
    feat_copy = pltpu.make_async_copy(feat_hbm, feat_ref, sems.at[0])
    k_copy = pltpu.make_async_copy(k_hbm, k_ref, sems.at[1])
    feat_copy.start()
    k_copy.start()
    feat_copy.wait()

    def slab(frame, row):
        if frame < frames:
            return (up_ref, own_ref, down_ref)[row][frame]
        return bnd_ref[row, frame - frames]

    def block(n):
        return slice(n * channels, (n + 1) * channels)

    lanes = lax.broadcasted_iota(jnp.int32, (channels, breadth), 1)
    for t in range(frames):
        values = feat_ref[t].astype(jnp.float32)
        active = (values * jax.nn.sigmoid(values)).astype(jnp.bfloat16).astype(jnp.float32)
        turned = active.T
        a_ref[t, block(0)] = jnp.where(lanes == 0, 0.0, pltpu.roll(turned, 1, 1)).astype(a_ref.dtype)
        a_ref[t, block(1)] = turned.astype(a_ref.dtype)
        a_ref[t, block(2)] = jnp.where(
            lanes == breadth - 1, 0.0, pltpu.roll(turned, breadth - 1, 1)
        ).astype(a_ref.dtype)
    k_copy.wait()
    for i in range(3):
        for j in range(3):
            for k in range(3):
                w_ref[j, block(k), block(i)] = k_ref[(i * 3 + j) * 3 + k]
    acc_ref[...] = jnp.zeros_like(acc_ref)
    rows = lax.broadcasted_iota(jnp.int32, (breadth, channels), 0)
    for t in range(frames):
        for j in range(3):
            for i in range(3):
                cat_ref[:, block(i)] = slab(t + 2 - i, 2 - j)
            joined = cat_ref[...]
            part = lax.dot_general(
                joined, w_ref[j], (((1,), (1,)), ((), ())), preferred_element_type=jnp.float32
            )
            if j == 0:
                z_ref[...] = part
            else:
                z_ref[...] += part
            acc_ref[j] += jnp.dot(a_ref[t], joined, preferred_element_type=jnp.float32)
        ahead = pltpu.roll(z_ref[:, block(0)], breadth - 1, 0)
        behind = pltpu.roll(z_ref[:, block(2)], 1, 0)
        grad_input = (
            jnp.where(rows == breadth - 1, 0.0, ahead)
            + z_ref[:, block(1)]
            + jnp.where(rows == 0, 0.0, behind)
        )
        values = feat_ref[t].astype(jnp.float32)
        sigmoid_part = jax.nn.sigmoid(values)
        derivative = sigmoid_part * (1.0 + values * (1.0 - sigmoid_part))
        gf_ref[t] = (own_ref[t].astype(jnp.float32) + derivative * grad_input).astype(gf_ref.dtype)
    for i in range(3):
        for j in range(3):
            term_ref[i * 3 + j] = acc_ref[j, :, block(i)] * factor


def local_grads(pieces, weights, feat, factor):
    frames, breadth, channels = feat.shape
    vmem = pl.BlockSpec(memory_space=pltpu.VMEM)
    operands = tuple(pieces) + (weights, feat)
    flops = 2 * 2 * frames * 9 * breadth * channels * 3 * channels
    moved = sum(2 * x.size for x in operands) + 2 * feat.size + 4 * 9 * 3 * channels * channels
    return pl.pallas_call(
        lambda *refs: local_kernel(factor, *refs),
        out_shape=(
            jax.ShapeDtypeStruct((frames, breadth, channels), jnp.bfloat16),
            jax.ShapeDtypeStruct((9, 3 * channels, channels), jnp.float32),
        ),
        in_specs=[vmem] * len(pieces) + [pl.BlockSpec(memory_space=pl.ANY)] * 2,
        out_specs=(vmem, vmem),
        scratch_shapes=[
            pltpu.VMEM((breadth, 3 * channels), jnp.float32),
            pltpu.VMEM((frames, 3 * channels, breadth), jnp.bfloat16),
            pltpu.VMEM((3, 3 * channels, 3 * channels), jnp.bfloat16),
            pltpu.VMEM((breadth, 3 * channels), jnp.bfloat16),
            pltpu.VMEM((3, 3 * channels, 3 * channels), jnp.float32),
            pltpu.VMEM(weights.shape, weights.dtype),
            pltpu.VMEM(feat.shape, feat.dtype),
            pltpu.SemaphoreType.DMA((2,)),
        ],
        compiler_params=pltpu.CompilerParams(vmem_limit_bytes=48 * 1024 * 1024),
        cost_estimate=pl.CostEstimate(flops=flops, bytes_accessed=moved, transcendentals=2 * feat.size),
    )(*operands)


def row_neighbours(x, axis):
    count = lax.axis_size(axis)
    up = [(i, i + 1) for i in range(count - 1)]
    down = [(j, i) for i, j in up]
    return lax.ppermute(x, axis, up), lax.ppermute(x, axis, down)


def body(features, cotangent, kernel):
    frames, height, breadth, channels = features.shape
    own = cotangent[:, 0]
    above, below = row_neighbours(own, "ha")
    boundary = passed_along(jnp.stack([above[:2], own[:2], below[:2]]), "ta", -1)
    total_cells = frames * height * breadth * lax.axis_size("ha") * lax.axis_size("ta")
    factor = float(total_cells) ** (-0.5)
    weights = kernel.reshape(-1, channels, channels)
    grad_features, term = local_grads((own, above, below, boundary), weights, features[:, 0], factor)
    term = term.reshape(-1, channels)
    owners = lax.axis_size("ha") * lax.axis_size("ta")
    rows = term.shape[0] // owners
    padded = -(-rows // 8) * 8
    term = jnp.pad(term.reshape(owners, rows, channels), ((0, 0), (0, padded - rows), (0, 0)))
    return (grad_features[:, None], term[None])


def physical_mesh(mesh):
    devices = mesh.devices
    coords = np.array([d.coords for d in devices.reshape(-1)])
    sizes = {"x": len(set(coords[:, 0])), "y": len(set(coords[:, 1])), "z": len(set(coords[:, 2]))}
    shape = tuple(sizes[a] for a in PHYSICAL) + (devices.shape[1],)
    grid = devices.reshape(shape)
    flat = np.array([d.coords for d in grid.reshape(-1)]).reshape(shape + (3,))
    want = np.stack(np.meshgrid(*[np.arange(n) for n in shape[:3]], indexing="ij"), -1)
    got = flat[..., 0, :][..., [1, 2, 0]]
    assert (got == want).all()
    return Mesh(grid, PHYSICAL + ("core",))


def reduce_blocks(term, order):
    rows = term.shape[2]
    part = term[0]
    for axis in order:
        count = lax.axis_size(axis)
        shaped = part.reshape((count, part.shape[0] // count) + part.shape[1:])
        if count == 2 and not isinstance(axis, tuple):
            first = lax.axis_index(axis) == 0
            kept = jnp.where(first, shaped[0], shaped[1])
            sent = jnp.where(first, shaped[1], shaped[0])
            part = kept + lax.ppermute(sent, axis, [(0, 1), (1, 0)])
        else:
            part = lax.all_to_all(shaped, axis, 0, 0, tiled=True).sum(0)
    return part[0]


def solution(mesh):
    placed = (P("ta", "ha", None, None), P("ta", "ha", None, None), P())
    local = jax.shard_map(
        body,
        mesh=mesh,
        in_specs=placed,
        out_specs=(P("ta", "ha", None, None), P(("ha", "ta"))),
        check_vma=False,
    )
    grid = physical_mesh(mesh)
    order = ("core", "y", "z", "x")
    stages = ("core", PHYSICAL)
    names = PHYSICAL + ("core",)
    sizes = [grid.shape[a] for a in names]

    def reorder(term):
        n, owners, padded, channels = term.shape
        t = term.reshape((n,) + tuple(sizes) + (padded, channels))
        perm = [0] + [1 + names.index(a) for a in order] + [5, 6]
        return t.transpose(perm).reshape(n, owners, padded, channels)

    def reduce_fn(term):
        rows = 27
        return reduce_blocks(term, order)

    rows_per = None

    def run(features, cotangent, kernel):
        grad_features, term = local(features, cotangent, kernel)
        channels = kernel.shape[-1]
        owners = term.shape[1]
        taps_rows = kernel.shape[0] * kernel.shape[1] * kernel.shape[2] * kernel.shape[3]
        rows = taps_rows // owners
        term = reorder(term)
        spec = P(names)
        part = jax.shard_map(
            lambda t: reduce_blocks(t, stages)[:rows],
            mesh=grid,
            in_specs=spec,
            out_specs=P(names),
            check_vma=False,
        )(term)
        part = lax.with_sharding_constraint(part, NamedSharding(mesh, P(("ha", "ta"), None)))
        return grad_features, part

    return run
```

```python
import jax
import jax.numpy as jnp
import numpy as np
from jax import lax
from jax.sharding import Mesh, NamedSharding
from jax.sharding import PartitionSpec as P
from jax.experimental import pallas as pl
from jax.experimental.pallas import tpu as pltpu

PHYSICAL = ("y", "z", "x")


def passed_along(block, axis, distance):
    devices = range(lax.axis_size(axis))
    route = [(i - distance, i) for i in devices if i - distance in devices]
    return lax.ppermute(block, axis, route)


def with_halo(x, sides, width):
    for axis, dim in sides:
        count, length = (lax.axis_size(axis), x.shape[dim])
        up = [(i, (i + 1) % count) for i in range(count - 1)]
        down = [(j, i) for i, j in up]
        last = lax.slice_in_dim(x, length - width, length, axis=dim)
        leading = lax.slice_in_dim(x, 0, width, axis=dim)
        before = lax.ppermute(last, axis, up)
        after = lax.ppermute(leading, axis, down)
        x = jnp.concatenate([before, x, after], axis=dim)
    return x


def local_kernel(factor, own_ref, up_ref, down_ref, bnd_ref, k_ref, feat_ref, gf_ref, term_ref, z_ref, a_ref, w_ref, cat_ref, acc_ref):
    frames, breadth, channels = feat_ref.shape

    def slab(frame, row):
        if frame < frames:
            return (up_ref, own_ref, down_ref)[row][frame]
        return bnd_ref[row, frame - frames]

    def block(n):
        return slice(n * channels, (n + 1) * channels)

    for i in range(3):
        for j in range(3):
            for k in range(3):
                w_ref[j, block(k), block(i)] = k_ref[(i * 3 + j) * 3 + k]
    lanes = lax.broadcasted_iota(jnp.int32, (channels, breadth), 1)
    for t in range(frames):
        values = feat_ref[t].astype(jnp.float32)
        active = (values * jax.nn.sigmoid(values)).astype(jnp.bfloat16).astype(jnp.float32)
        turned = active.T
        a_ref[t, block(0)] = jnp.where(lanes == 0, 0.0, pltpu.roll(turned, 1, 1)).astype(a_ref.dtype)
        a_ref[t, block(1)] = turned.astype(a_ref.dtype)
        a_ref[t, block(2)] = jnp.where(
            lanes == breadth - 1, 0.0, pltpu.roll(turned, breadth - 1, 1)
        ).astype(a_ref.dtype)
    acc_ref[...] = jnp.zeros_like(acc_ref)
    rows = lax.broadcasted_iota(jnp.int32, (breadth, channels), 0)
    for t in range(frames):
        for j in range(3):
            for i in range(3):
                cat_ref[:, block(i)] = slab(t + 2 - i, 2 - j)
            joined = cat_ref[...]
            part = lax.dot_general(
                joined, w_ref[j], (((1,), (1,)), ((), ())), preferred_element_type=jnp.float32
            )
            if j == 0:
                z_ref[...] = part
            else:
                z_ref[...] += part
            acc_ref[j] += jnp.dot(a_ref[t], joined, preferred_element_type=jnp.float32)
        ahead = pltpu.roll(z_ref[:, block(0)], breadth - 1, 0)
        behind = pltpu.roll(z_ref[:, block(2)], 1, 0)
        grad_input = (
            jnp.where(rows == breadth - 1, 0.0, ahead)
            + z_ref[:, block(1)]
            + jnp.where(rows == 0, 0.0, behind)
        )
        values = feat_ref[t].astype(jnp.float32)
        sigmoid_part = jax.nn.sigmoid(values)
        derivative = sigmoid_part * (1.0 + values * (1.0 - sigmoid_part))
        gf_ref[t] = (own_ref[t].astype(jnp.float32) + derivative * grad_input).astype(gf_ref.dtype)
    for i in range(3):
        for j in range(3):
            term_ref[i * 3 + j] = acc_ref[j, :, block(i)] * factor


def local_grads(pieces, weights, feat, factor):
    frames, breadth, channels = feat.shape
    vmem = pl.BlockSpec(memory_space=pltpu.VMEM)
    operands = tuple(pieces) + (weights, feat)
    flops = 2 * 2 * frames * 9 * breadth * channels * 3 * channels
    moved = sum(2 * x.size for x in operands) + 2 * feat.size + 4 * 9 * 3 * channels * channels
    return pl.pallas_call(
        lambda *refs: local_kernel(factor, *refs),
        out_shape=(
            jax.ShapeDtypeStruct((frames, breadth, channels), jnp.bfloat16),
            jax.ShapeDtypeStruct((9, 3 * channels, channels), jnp.float32),
        ),
        in_specs=[vmem] * len(operands),
        out_specs=(vmem, vmem),
        scratch_shapes=[
            pltpu.VMEM((breadth, 3 * channels), jnp.float32),
            pltpu.VMEM((frames, 3 * channels, breadth), jnp.bfloat16),
            pltpu.VMEM((3, 3 * channels, 3 * channels), jnp.bfloat16),
            pltpu.VMEM((breadth, 3 * channels), jnp.bfloat16),
            pltpu.VMEM((3, 3 * channels, 3 * channels), jnp.float32),
        ],
        compiler_params=pltpu.CompilerParams(vmem_limit_bytes=48 * 1024 * 1024),
        cost_estimate=pl.CostEstimate(flops=flops, bytes_accessed=moved, transcendentals=2 * feat.size),
    )(*operands)


def row_neighbours(x, axis):
    count = lax.axis_size(axis)
    up = [(i, i + 1) for i in range(count - 1)]
    down = [(j, i) for i, j in up]
    return lax.ppermute(x, axis, up), lax.ppermute(x, axis, down)


def body(features, cotangent, kernel):
    frames, height, breadth, channels = features.shape
    own = cotangent[:, 0]
    above, below = row_neighbours(own, "ha")
    boundary = passed_along(jnp.stack([above[:2], own[:2], below[:2]]), "ta", -1)
    total_cells = frames * height * breadth * lax.axis_size("ha") * lax.axis_size("ta")
    factor = float(total_cells) ** (-0.5)
    weights = kernel.reshape(-1, channels, channels)
    grad_features, term = local_grads((own, above, below, boundary), weights, features[:, 0], factor)
    term = term.reshape(-1, channels)
    owners = lax.axis_size("ha") * lax.axis_size("ta")
    rows = term.shape[0] // owners
    return (grad_features[:, None], term.reshape(owners, rows * channels)[None])


def physical_mesh(mesh):
    devices = mesh.devices
    coords = np.array([d.coords for d in devices.reshape(-1)])
    sizes = {"x": len(set(coords[:, 0])), "y": len(set(coords[:, 1])), "z": len(set(coords[:, 2]))}
    shape = tuple(sizes[a] for a in PHYSICAL) + (devices.shape[1],)
    grid = devices.reshape(shape)
    flat = np.array([d.coords for d in grid.reshape(-1)]).reshape(shape + (3,))
    want = np.stack(np.meshgrid(*[np.arange(n) for n in shape[:3]], indexing="ij"), -1)
    got = flat[..., 0, :][..., [1, 2, 0]]
    assert (got == want).all()
    return Mesh(grid, PHYSICAL + ("core",))


def reduce_blocks(term, order):
    rows = term.shape[2]
    part = term[0]
    for axis in order:
        count = lax.axis_size(axis)
        shaped = part.reshape((count, part.shape[0] // count) + part.shape[1:])
        part = lax.all_to_all(shaped, axis, 0, 0, tiled=True).sum(0)
    return part[0]


def solution(mesh):
    placed = (P("ta", "ha", None, None), P("ta", "ha", None, None), P())
    local = jax.shard_map(
        body,
        mesh=mesh,
        in_specs=placed,
        out_specs=(P("ta", "ha", None, None), P(("ha", "ta"))),
        check_vma=False,
    )
    grid = physical_mesh(mesh)
    order = ("core", "y", "z", "x")
    stages = ("core", PHYSICAL)
    names = PHYSICAL + ("core",)
    sizes = [grid.shape[a] for a in names]

    def reorder(term):
        n, owners = term.shape[:2]
        t = term.reshape((n,) + tuple(sizes) + term.shape[2:])
        perm = [0] + [1 + names.index(a) for a in order] + list(range(5, t.ndim))
        return t.transpose(perm).reshape(term.shape)

    def reduce_fn(term):
        rows = 27
        return reduce_blocks(term, order)

    rows_per = None

    def run(features, cotangent, kernel):
        grad_features, term = local(features, cotangent, kernel)
        channels = kernel.shape[-1]
        owners = term.shape[1]
        taps_rows = kernel.shape[0] * kernel.shape[1] * kernel.shape[2] * kernel.shape[3]
        rows = taps_rows // owners
        term = reorder(term)
        spec = P(names)
        part = jax.shard_map(
            lambda t: reduce_blocks(t, stages).reshape(rows, channels),
            mesh=grid,
            in_specs=spec,
            out_specs=P(names),
            check_vma=False,
        )(term)
        part = lax.with_sharding_constraint(part, NamedSharding(mesh, P(("ha", "ta"), None)))
        return grad_features, part

    return run
```

```python
import jax
import jax.numpy as jnp
import numpy as np
from jax import lax
from jax.sharding import Mesh, NamedSharding
from jax.sharding import PartitionSpec as P
from jax.experimental import pallas as pl
from jax.experimental.pallas import tpu as pltpu

PHYSICAL = ("y", "z", "x")


def passed_along(block, axis, distance):
    devices = range(lax.axis_size(axis))
    route = [(i - distance, i) for i in devices if i - distance in devices]
    return lax.ppermute(block, axis, route)


def with_halo(x, sides, width):
    for axis, dim in sides:
        count, length = (lax.axis_size(axis), x.shape[dim])
        up = [(i, (i + 1) % count) for i in range(count - 1)]
        down = [(j, i) for i, j in up]
        last = lax.slice_in_dim(x, length - width, length, axis=dim)
        leading = lax.slice_in_dim(x, 0, width, axis=dim)
        before = lax.ppermute(last, axis, up)
        after = lax.ppermute(leading, axis, down)
        x = jnp.concatenate([before, x, after], axis=dim)
    return x


def local_kernel(factor, own_ref, up_ref, down_ref, late_up_ref, late_own_ref, late_down_ref, k_ref, feat_ref, gf_ref, term_ref, z_ref, a_ref, w_ref, cat_ref, acc_ref):
    frames, breadth, channels = feat_ref.shape

    def slab(frame, row):
        if frame < frames:
            return (up_ref, own_ref, down_ref)[row][frame]
        return (late_up_ref, late_own_ref, late_down_ref)[row][frame - frames]

    def block(n):
        return slice(n * channels, (n + 1) * channels)

    for i in range(3):
        for j in range(3):
            for k in range(3):
                w_ref[j, block(k), block(i)] = k_ref[(i * 3 + j) * 3 + k]
    lanes = lax.broadcasted_iota(jnp.int32, (channels, breadth), 1)
    for t in range(frames):
        values = feat_ref[t].astype(jnp.float32)
        active = (values * jax.nn.sigmoid(values)).astype(jnp.bfloat16).astype(jnp.float32)
        turned = active.T
        a_ref[t, block(0)] = jnp.where(lanes == 0, 0.0, pltpu.roll(turned, 1, 1)).astype(a_ref.dtype)
        a_ref[t, block(1)] = turned.astype(a_ref.dtype)
        a_ref[t, block(2)] = jnp.where(
            lanes == breadth - 1, 0.0, pltpu.roll(turned, breadth - 1, 1)
        ).astype(a_ref.dtype)
    acc_ref[...] = jnp.zeros_like(acc_ref)
    rows = lax.broadcasted_iota(jnp.int32, (breadth, channels), 0)
    for t in range(frames):
        for j in range(3):
            for i in range(3):
                cat_ref[:, block(i)] = slab(t + 2 - i, 2 - j)
            joined = cat_ref[...]
            part = lax.dot_general(
                joined, w_ref[j], (((1,), (1,)), ((), ())), preferred_element_type=jnp.float32
            )
            if j == 0:
                z_ref[...] = part
            else:
                z_ref[...] += part
            acc_ref[j] += jnp.dot(a_ref[t], joined, preferred_element_type=jnp.float32)
        ahead = pltpu.roll(z_ref[:, block(0)], breadth - 1, 0)
        behind = pltpu.roll(z_ref[:, block(2)], 1, 0)
        grad_input = (
            jnp.where(rows == breadth - 1, 0.0, ahead)
            + z_ref[:, block(1)]
            + jnp.where(rows == 0, 0.0, behind)
        )
        values = feat_ref[t].astype(jnp.float32)
        sigmoid_part = jax.nn.sigmoid(values)
        derivative = sigmoid_part * (1.0 + values * (1.0 - sigmoid_part))
        gf_ref[t] = (own_ref[t].astype(jnp.float32) + derivative * grad_input).astype(gf_ref.dtype)
    for i in range(3):
        for j in range(3):
            term_ref[i * 3 + j] = acc_ref[j, :, block(i)] * factor


def local_grads(pieces, weights, feat, factor):
    frames, breadth, channels = feat.shape
    vmem = pl.BlockSpec(memory_space=pltpu.VMEM)
    operands = tuple(pieces) + (weights, feat)
    flops = 2 * 2 * frames * 9 * breadth * channels * 3 * channels
    moved = sum(2 * x.size for x in operands) + 2 * feat.size + 4 * 9 * 3 * channels * channels
    return pl.pallas_call(
        lambda *refs: local_kernel(factor, *refs),
        out_shape=(
            jax.ShapeDtypeStruct((frames, breadth, channels), jnp.bfloat16),
            jax.ShapeDtypeStruct((9, 3 * channels, channels), jnp.float32),
        ),
        in_specs=[vmem] * len(operands),
        out_specs=(vmem, vmem),
        scratch_shapes=[
            pltpu.VMEM((breadth, 3 * channels), jnp.float32),
            pltpu.VMEM((frames, 3 * channels, breadth), jnp.bfloat16),
            pltpu.VMEM((3, 3 * channels, 3 * channels), jnp.bfloat16),
            pltpu.VMEM((breadth, 3 * channels), jnp.bfloat16),
            pltpu.VMEM((3, 3 * channels, 3 * channels), jnp.float32),
        ],
        compiler_params=pltpu.CompilerParams(vmem_limit_bytes=48 * 1024 * 1024),
        cost_estimate=pl.CostEstimate(flops=flops, bytes_accessed=moved, transcendentals=2 * feat.size),
    )(*operands)


def row_neighbours(x, axis):
    count = lax.axis_size(axis)
    up = [(i, i + 1) for i in range(count - 1)]
    down = [(j, i) for i, j in up]
    return lax.ppermute(x, axis, up), lax.ppermute(x, axis, down)


def body(features, cotangent, kernel):
    frames, height, breadth, channels = features.shape
    own = cotangent[:, 0]
    above, below = row_neighbours(own, "ha")
    early = own[:2]
    joint = ("ha", "ta")
    rows_count, cores = lax.axis_size("ha"), lax.axis_size("ta")
    late_up = lax.ppermute(early, joint, [((h - 1) * cores + 1, h * cores) for h in range(1, rows_count)])
    late_down = lax.ppermute(early, joint, [((h + 1) * cores + 1, h * cores) for h in range(rows_count - 1)])
    late_own = passed_along(early, "ta", -1)
    total_cells = frames * height * breadth * lax.axis_size("ha") * lax.axis_size("ta")
    factor = float(total_cells) ** (-0.5)
    weights = kernel.reshape(-1, channels, channels)
    grad_features, term = local_grads((own, above, below, late_up, late_own, late_down), weights, features[:, 0], factor)
    term = term.reshape(-1, channels)
    owners = lax.axis_size("ha") * lax.axis_size("ta")
    rows = term.shape[0] // owners
    return (grad_features[:, None], term.reshape(owners, rows * channels)[None])


def physical_mesh(mesh):
    devices = mesh.devices
    coords = np.array([d.coords for d in devices.reshape(-1)])
    sizes = {"x": len(set(coords[:, 0])), "y": len(set(coords[:, 1])), "z": len(set(coords[:, 2]))}
    shape = tuple(sizes[a] for a in PHYSICAL) + (devices.shape[1],)
    grid = devices.reshape(shape)
    flat = np.array([d.coords for d in grid.reshape(-1)]).reshape(shape + (3,))
    want = np.stack(np.meshgrid(*[np.arange(n) for n in shape[:3]], indexing="ij"), -1)
    got = flat[..., 0, :][..., [1, 2, 0]]
    assert (got == want).all()
    return Mesh(grid, PHYSICAL + ("core",))


def reduce_blocks(term, order):
    rows = term.shape[2]
    part = term[0]
    for axis in order:
        count = lax.axis_size(axis)
        shaped = part.reshape((count, part.shape[0] // count) + part.shape[1:])
        part = lax.all_to_all(shaped, axis, 0, 0, tiled=True).sum(0)
    return part[0]


def solution(mesh):
    placed = (P("ta", "ha", None, None), P("ta", "ha", None, None), P())
    local = jax.shard_map(
        body,
        mesh=mesh,
        in_specs=placed,
        out_specs=(P("ta", "ha", None, None), P(("ha", "ta"))),
        check_vma=False,
    )
    grid = physical_mesh(mesh)
    order = ("core", "y", "z", "x")
    stages = ("core", PHYSICAL)
    names = PHYSICAL + ("core",)
    sizes = [grid.shape[a] for a in names]

    def reorder(term):
        n, owners = term.shape[:2]
        t = term.reshape((n,) + tuple(sizes) + term.shape[2:])
        perm = [0] + [1 + names.index(a) for a in order] + list(range(5, t.ndim))
        return t.transpose(perm).reshape(term.shape)

    def reduce_fn(term):
        rows = 27
        return reduce_blocks(term, order)

    rows_per = None

    def run(features, cotangent, kernel):
        grad_features, term = local(features, cotangent, kernel)
        channels = kernel.shape[-1]
        owners = term.shape[1]
        taps_rows = kernel.shape[0] * kernel.shape[1] * kernel.shape[2] * kernel.shape[3]
        rows = taps_rows // owners
        term = reorder(term)
        spec = P(names)
        part = jax.shard_map(
            lambda t: reduce_blocks(t, stages).reshape(rows, channels),
            mesh=grid,
            in_specs=spec,
            out_specs=P(names),
            check_vma=False,
        )(term)
        part = lax.with_sharding_constraint(part, NamedSharding(mesh, P(("ha", "ta"), None)))
        return grad_features, part

    return run
```

```python
import jax
import jax.numpy as jnp
import numpy as np
from jax import lax
from jax.sharding import Mesh, NamedSharding
from jax.sharding import PartitionSpec as P
from jax.experimental import pallas as pl
from jax.experimental.pallas import tpu as pltpu

PHYSICAL = ("y", "z", "x")


def passed_along(block, axis, distance):
    devices = range(lax.axis_size(axis))
    route = [(i - distance, i) for i in devices if i - distance in devices]
    return lax.ppermute(block, axis, route)


def with_halo(x, sides, width):
    for axis, dim in sides:
        count, length = (lax.axis_size(axis), x.shape[dim])
        up = [(i, (i + 1) % count) for i in range(count - 1)]
        down = [(j, i) for i, j in up]
        last = lax.slice_in_dim(x, length - width, length, axis=dim)
        leading = lax.slice_in_dim(x, 0, width, axis=dim)
        before = lax.ppermute(last, axis, up)
        after = lax.ppermute(leading, axis, down)
        x = jnp.concatenate([before, x, after], axis=dim)
    return x


def local_kernel(factor, own_ref, up_ref, down_ref, late_up_ref, late_own_ref, late_down_ref, k_ref, feat_ref, gf_ref, term_ref, z_ref, a_ref, w_ref, cat_ref, acc_ref):
    frames, breadth, channels = feat_ref.shape

    def slab(frame, row):
        if frame < frames:
            return (up_ref, own_ref, down_ref)[row][frame]
        return (late_up_ref, late_own_ref, late_down_ref)[row][frame - frames]

    def block(n):
        return slice(n * channels, (n + 1) * channels)

    for i in range(3):
        for j in range(3):
            for k in range(3):
                w_ref[j, block(k), block(i)] = k_ref[(i * 3 + j) * 3 + k]
    lanes = lax.broadcasted_iota(jnp.int32, (channels, breadth), 1)
    for t in range(frames):
        values = feat_ref[t].astype(jnp.float32)
        active = (values * jax.nn.sigmoid(values)).astype(jnp.bfloat16).astype(jnp.float32)
        turned = active.T
        a_ref[t, block(0)] = jnp.where(lanes == 0, 0.0, pltpu.roll(turned, 1, 1)).astype(a_ref.dtype)
        a_ref[t, block(1)] = turned.astype(a_ref.dtype)
        a_ref[t, block(2)] = jnp.where(
            lanes == breadth - 1, 0.0, pltpu.roll(turned, breadth - 1, 1)
        ).astype(a_ref.dtype)
    acc_ref[...] = jnp.zeros_like(acc_ref)
    rows = lax.broadcasted_iota(jnp.int32, (breadth, channels), 0)
    for t in range(frames):
        for j in range(3):
            for i in range(3):
                cat_ref[:, block(i)] = slab(t + 2 - i, 2 - j)
            joined = cat_ref[...]
            part = lax.dot_general(
                joined, w_ref[j], (((1,), (1,)), ((), ())), preferred_element_type=jnp.float32
            )
            if j == 0:
                z_ref[...] = part
            else:
                z_ref[...] += part
            acc_ref[j] += jnp.dot(a_ref[t], joined, preferred_element_type=jnp.float32)
        ahead = pltpu.roll(z_ref[:, block(0)], breadth - 1, 0)
        behind = pltpu.roll(z_ref[:, block(2)], 1, 0)
        grad_input = (
            jnp.where(rows == breadth - 1, 0.0, ahead)
            + z_ref[:, block(1)]
            + jnp.where(rows == 0, 0.0, behind)
        )
        values = feat_ref[t].astype(jnp.float32)
        sigmoid_part = jax.nn.sigmoid(values)
        derivative = sigmoid_part * (1.0 + values * (1.0 - sigmoid_part))
        gf_ref[t] = (own_ref[t].astype(jnp.float32) + derivative * grad_input).astype(gf_ref.dtype)
    for i in range(3):
        for j in range(3):
            term_ref[i * 3 + j] = acc_ref[j, :, block(i)] * factor


def local_grads(pieces, weights, feat, factor):
    frames, breadth, channels = feat.shape
    vmem = pl.BlockSpec(memory_space=pltpu.VMEM)
    operands = tuple(pieces) + (weights, feat)
    flops = 2 * 2 * frames * 9 * breadth * channels * 3 * channels
    moved = sum(2 * x.size for x in operands) + 2 * feat.size + 4 * 9 * 3 * channels * channels
    return pl.pallas_call(
        lambda *refs: local_kernel(factor, *refs),
        out_shape=(
            jax.ShapeDtypeStruct((frames, breadth, channels), jnp.bfloat16),
            jax.ShapeDtypeStruct((9, 3 * channels, channels), jnp.float32),
        ),
        in_specs=[vmem] * len(operands),
        out_specs=(vmem, vmem),
        scratch_shapes=[
            pltpu.VMEM((breadth, 3 * channels), jnp.float32),
            pltpu.VMEM((frames, 3 * channels, breadth), jnp.bfloat16),
            pltpu.VMEM((3, 3 * channels, 3 * channels), jnp.bfloat16),
            pltpu.VMEM((breadth, 3 * channels), jnp.bfloat16),
            pltpu.VMEM((3, 3 * channels, 3 * channels), jnp.float32),
        ],
        compiler_params=pltpu.CompilerParams(vmem_limit_bytes=60 * 1024 * 1024),
        cost_estimate=pl.CostEstimate(flops=flops, bytes_accessed=moved, transcendentals=2 * feat.size),
    )(*operands)


def row_neighbours(x, axis):
    count = lax.axis_size(axis)
    up = [(i, i + 1) for i in range(count - 1)]
    down = [(j, i) for i, j in up]
    return lax.ppermute(x, axis, up), lax.ppermute(x, axis, down)


def body(features, cotangent, kernel):
    frames, height, breadth, channels = features.shape
    own = cotangent[:, 0]
    above, below = row_neighbours(own, "ha")
    early = own[:2]
    joint = ("ha", "ta")
    rows_count, cores = lax.axis_size("ha"), lax.axis_size("ta")
    late_up = lax.ppermute(early, joint, [((h - 1) * cores + 1, h * cores) for h in range(1, rows_count)])
    late_down = lax.ppermute(early, joint, [((h + 1) * cores + 1, h * cores) for h in range(rows_count - 1)])
    late_own = passed_along(early, "ta", -1)
    total_cells = frames * height * breadth * lax.axis_size("ha") * lax.axis_size("ta")
    factor = float(total_cells) ** (-0.5)
    weights = kernel.reshape(-1, channels, channels)
    grad_features, term = local_grads((own, above, below, late_up, late_own, late_down), weights, features[:, 0], factor)
    term = term.reshape(-1, channels)
    owners = lax.axis_size("ha") * lax.axis_size("ta")
    rows = term.shape[0] // owners
    return (grad_features[:, None], term.reshape(owners, rows * channels)[None])


def physical_mesh(mesh):
    devices = mesh.devices
    coords = np.array([d.coords for d in devices.reshape(-1)])
    sizes = {"x": len(set(coords[:, 0])), "y": len(set(coords[:, 1])), "z": len(set(coords[:, 2]))}
    shape = tuple(sizes[a] for a in PHYSICAL) + (devices.shape[1],)
    grid = devices.reshape(shape)
    flat = np.array([d.coords for d in grid.reshape(-1)]).reshape(shape + (3,))
    want = np.stack(np.meshgrid(*[np.arange(n) for n in shape[:3]], indexing="ij"), -1)
    got = flat[..., 0, :][..., [1, 2, 0]]
    assert (got == want).all()
    return Mesh(grid, PHYSICAL + ("core",))


def reduce_blocks(term, order):
    rows = term.shape[2]
    part = term[0]
    for axis in order:
        count = lax.axis_size(axis)
        shaped = part.reshape((count, part.shape[0] // count) + part.shape[1:])
        part = lax.all_to_all(shaped, axis, 0, 0, tiled=True).sum(0)
    return part[0]


def solution(mesh):
    placed = (P("ta", "ha", None, None), P("ta", "ha", None, None), P())
    local = jax.shard_map(
        body,
        mesh=mesh,
        in_specs=placed,
        out_specs=(P("ta", "ha", None, None), P(("ha", "ta"))),
        check_vma=False,
    )
    grid = physical_mesh(mesh)
    order = ("core", "y", "z", "x")
    stages = ("core", PHYSICAL)
    names = PHYSICAL + ("core",)
    sizes = [grid.shape[a] for a in names]

    def reorder(term):
        n, owners = term.shape[:2]
        t = term.reshape((n,) + tuple(sizes) + term.shape[2:])
        perm = [0] + [1 + names.index(a) for a in order] + list(range(5, t.ndim))
        return t.transpose(perm).reshape(term.shape)

    def reduce_fn(term):
        rows = 27
        return reduce_blocks(term, order)

    rows_per = None

    def run(features, cotangent, kernel):
        grad_features, term = local(features, cotangent, kernel)
        channels = kernel.shape[-1]
        owners = term.shape[1]
        taps_rows = kernel.shape[0] * kernel.shape[1] * kernel.shape[2] * kernel.shape[3]
        rows = taps_rows // owners
        term = reorder(term)
        spec = P(names)
        part = jax.shard_map(
            lambda t: reduce_blocks(t, stages).reshape(rows, channels),
            mesh=grid,
            in_specs=spec,
            out_specs=P(names),
            check_vma=False,
        )(term)
        part = lax.with_sharding_constraint(part, NamedSharding(mesh, P(("ha", "ta"), None)))
        return grad_features, part

    return run
```

```python
import jax
import jax.numpy as jnp
import numpy as np
from jax import lax
from jax.sharding import Mesh, NamedSharding
from jax.sharding import PartitionSpec as P
from jax.experimental import pallas as pl
from jax.experimental.pallas import tpu as pltpu

PHYSICAL = ("y", "z", "x")


def passed_along(block, axis, distance):
    devices = range(lax.axis_size(axis))
    route = [(i - distance, i) for i in devices if i - distance in devices]
    return lax.ppermute(block, axis, route)


def with_halo(x, sides, width):
    for axis, dim in sides:
        count, length = (lax.axis_size(axis), x.shape[dim])
        up = [(i, (i + 1) % count) for i in range(count - 1)]
        down = [(j, i) for i, j in up]
        last = lax.slice_in_dim(x, length - width, length, axis=dim)
        leading = lax.slice_in_dim(x, 0, width, axis=dim)
        before = lax.ppermute(last, axis, up)
        after = lax.ppermute(leading, axis, down)
        x = jnp.concatenate([before, x, after], axis=dim)
    return x


def local_kernel(factor, own_ref, up_ref, down_ref, bnd_ref, k_ref, feat_ref, gf_ref, term_ref, z_ref, a_ref, w_ref, cat_ref, acc_ref, s_ref):
    frames, breadth, channels = feat_ref.shape

    def slab(frame, row):
        if frame < frames:
            return (up_ref, own_ref, down_ref)[row][frame]
        return bnd_ref[row, frame - frames]

    def block(n):
        return slice(n * channels, (n + 1) * channels)

    for i in range(3):
        for j in range(3):
            for k in range(3):
                w_ref[j, block(k), block(i)] = k_ref[(i * 3 + j) * 3 + k]
    lanes = lax.broadcasted_iota(jnp.int32, (channels, breadth), 1)
    for t in range(frames):
        values = feat_ref[t].astype(jnp.float32)
        s_ref[t] = jax.nn.sigmoid(values)
        active = (values * s_ref[t]).astype(jnp.bfloat16).astype(jnp.float32)
        turned = active.T
        a_ref[t, block(0)] = jnp.where(lanes == 0, 0.0, pltpu.roll(turned, 1, 1)).astype(a_ref.dtype)
        a_ref[t, block(1)] = turned.astype(a_ref.dtype)
        a_ref[t, block(2)] = jnp.where(
            lanes == breadth - 1, 0.0, pltpu.roll(turned, breadth - 1, 1)
        ).astype(a_ref.dtype)
    acc_ref[...] = jnp.zeros_like(acc_ref)
    rows = lax.broadcasted_iota(jnp.int32, (breadth, channels), 0)
    for t in range(frames):
        for j in range(3):
            for i in range(3):
                cat_ref[:, block(i)] = slab(t + 2 - i, 2 - j)
            joined = cat_ref[...]
            part = lax.dot_general(
                joined, w_ref[j], (((1,), (1,)), ((), ())), preferred_element_type=jnp.float32
            )
            if j == 0:
                z_ref[...] = part
            else:
                z_ref[...] += part
            acc_ref[j] += jnp.dot(a_ref[t], joined, preferred_element_type=jnp.float32)
        ahead = pltpu.roll(z_ref[:, block(0)], breadth - 1, 0)
        behind = pltpu.roll(z_ref[:, block(2)], 1, 0)
        grad_input = (
            jnp.where(rows == breadth - 1, 0.0, ahead)
            + z_ref[:, block(1)]
            + jnp.where(rows == 0, 0.0, behind)
        )
        values = feat_ref[t].astype(jnp.float32)
        sigmoid_part = s_ref[t]
        derivative = sigmoid_part * (1.0 + values * (1.0 - sigmoid_part))
        gf_ref[t] = (own_ref[t].astype(jnp.float32) + derivative * grad_input).astype(gf_ref.dtype)
    for i in range(3):
        for j in range(3):
            term_ref[i * 3 + j] = acc_ref[j, :, block(i)] * factor


def local_grads(pieces, weights, feat, factor):
    frames, breadth, channels = feat.shape
    vmem = pl.BlockSpec(memory_space=pltpu.VMEM)
    operands = tuple(pieces) + (weights, feat)
    flops = 2 * 2 * frames * 9 * breadth * channels * 3 * channels
    moved = sum(2 * x.size for x in operands) + 2 * feat.size + 4 * 9 * 3 * channels * channels
    return pl.pallas_call(
        lambda *refs: local_kernel(factor, *refs),
        out_shape=(
            jax.ShapeDtypeStruct((frames, breadth, channels), jnp.bfloat16),
            jax.ShapeDtypeStruct((9, 3 * channels, channels), jnp.float32),
        ),
        in_specs=[vmem] * len(operands),
        out_specs=(vmem, vmem),
        scratch_shapes=[
            pltpu.VMEM((breadth, 3 * channels), jnp.float32),
            pltpu.VMEM((frames, 3 * channels, breadth), jnp.bfloat16),
            pltpu.VMEM((3, 3 * channels, 3 * channels), jnp.bfloat16),
            pltpu.VMEM((breadth, 3 * channels), jnp.bfloat16),
            pltpu.VMEM((3, 3 * channels, 3 * channels), jnp.float32),
            pltpu.VMEM((frames, breadth, channels), jnp.float32),
        ],
        compiler_params=pltpu.CompilerParams(vmem_limit_bytes=48 * 1024 * 1024),
        cost_estimate=pl.CostEstimate(flops=flops, bytes_accessed=moved, transcendentals=2 * feat.size),
    )(*operands)


def row_neighbours(x, axis):
    count = lax.axis_size(axis)
    up = [(i, i + 1) for i in range(count - 1)]
    down = [(j, i) for i, j in up]
    return lax.ppermute(x, axis, up), lax.ppermute(x, axis, down)


def body(features, cotangent, kernel):
    frames, height, breadth, channels = features.shape
    own = cotangent[:, 0]
    above, below = row_neighbours(own, "ha")
    boundary = passed_along(jnp.stack([above[:2], own[:2], below[:2]]), "ta", -1)
    total_cells = frames * height * breadth * lax.axis_size("ha") * lax.axis_size("ta")
    factor = float(total_cells) ** (-0.5)
    weights = kernel.reshape(-1, channels, channels)
    grad_features, term = local_grads((own, above, below, boundary), weights, features[:, 0], factor)
    term = term.reshape(-1, channels)
    owners = lax.axis_size("ha") * lax.axis_size("ta")
    rows = term.shape[0] // owners
    return (grad_features[:, None], term.reshape(owners, rows * channels)[None])


def physical_mesh(mesh):
    devices = mesh.devices
    coords = np.array([d.coords for d in devices.reshape(-1)])
    sizes = {"x": len(set(coords[:, 0])), "y": len(set(coords[:, 1])), "z": len(set(coords[:, 2]))}
    shape = tuple(sizes[a] for a in PHYSICAL) + (devices.shape[1],)
    grid = devices.reshape(shape)
    flat = np.array([d.coords for d in grid.reshape(-1)]).reshape(shape + (3,))
    want = np.stack(np.meshgrid(*[np.arange(n) for n in shape[:3]], indexing="ij"), -1)
    got = flat[..., 0, :][..., [1, 2, 0]]
    assert (got == want).all()
    return Mesh(grid, PHYSICAL + ("core",))


def reduce_blocks(term, order):
    rows = term.shape[2]
    part = term[0]
    for axis in order:
        count = lax.axis_size(axis)
        shaped = part.reshape((count, part.shape[0] // count) + part.shape[1:])
        part = lax.all_to_all(shaped, axis, 0, 0, tiled=True).sum(0)
    return part[0]


def solution(mesh):
    placed = (P("ta", "ha", None, None), P("ta", "ha", None, None), P())
    local = jax.shard_map(
        body,
        mesh=mesh,
        in_specs=placed,
        out_specs=(P("ta", "ha", None, None), P(("ha", "ta"))),
        check_vma=False,
    )
    grid = physical_mesh(mesh)
    order = ("core", "y", "z", "x")
    stages = ("core", PHYSICAL)
    names = PHYSICAL + ("core",)
    sizes = [grid.shape[a] for a in names]

    def reorder(term):
        n, owners = term.shape[:2]
        t = term.reshape((n,) + tuple(sizes) + term.shape[2:])
        perm = [0] + [1 + names.index(a) for a in order] + list(range(5, t.ndim))
        return t.transpose(perm).reshape(term.shape)

    def reduce_fn(term):
        rows = 27
        return reduce_blocks(term, order)

    rows_per = None

    def run(features, cotangent, kernel):
        grad_features, term = local(features, cotangent, kernel)
        channels = kernel.shape[-1]
        owners = term.shape[1]
        taps_rows = kernel.shape[0] * kernel.shape[1] * kernel.shape[2] * kernel.shape[3]
        rows = taps_rows // owners
        term = reorder(term)
        spec = P(names)
        part = jax.shard_map(
            lambda t: reduce_blocks(t, stages).reshape(rows, channels),
            mesh=grid,
            in_specs=spec,
            out_specs=P(names),
            check_vma=False,
        )(term)
        part = lax.with_sharding_constraint(part, NamedSharding(mesh, P(("ha", "ta"), None)))
        return grad_features, part

    return run
```

```python
import jax
import jax.numpy as jnp
import numpy as np
from jax import lax
from jax.sharding import Mesh, NamedSharding
from jax.sharding import PartitionSpec as P
from jax.experimental import pallas as pl
from jax.experimental.pallas import tpu as pltpu

PHYSICAL = ("y", "z", "x")


def passed_along(block, axis, distance):
    devices = range(lax.axis_size(axis))
    route = [(i - distance, i) for i in devices if i - distance in devices]
    return lax.ppermute(block, axis, route)


def with_halo(x, sides, width):
    for axis, dim in sides:
        count, length = (lax.axis_size(axis), x.shape[dim])
        up = [(i, (i + 1) % count) for i in range(count - 1)]
        down = [(j, i) for i, j in up]
        last = lax.slice_in_dim(x, length - width, length, axis=dim)
        leading = lax.slice_in_dim(x, 0, width, axis=dim)
        before = lax.ppermute(last, axis, up)
        after = lax.ppermute(leading, axis, down)
        x = jnp.concatenate([before, x, after], axis=dim)
    return x


def prep_kernel(k_ref, feat_ref, a_ref, w_ref):
    frames, breadth, channels = feat_ref.shape

    def block(n):
        return slice(n * channels, (n + 1) * channels)

    for i in range(3):
        for j in range(3):
            for k in range(3):
                w_ref[j, block(k), block(i)] = k_ref[(i * 3 + j) * 3 + k]
    lanes = lax.broadcasted_iota(jnp.int32, (channels, breadth), 1)
    for t in range(frames):
        values = feat_ref[t].astype(jnp.float32)
        active = (values * jax.nn.sigmoid(values)).astype(jnp.bfloat16).astype(jnp.float32)
        turned = active.T
        a_ref[t, block(0)] = jnp.where(lanes == 0, 0.0, pltpu.roll(turned, 1, 1)).astype(a_ref.dtype)
        a_ref[t, block(1)] = turned.astype(a_ref.dtype)
        a_ref[t, block(2)] = jnp.where(
            lanes == breadth - 1, 0.0, pltpu.roll(turned, breadth - 1, 1)
        ).astype(a_ref.dtype)


def local_kernel(factor, own_ref, up_ref, down_ref, bnd_ref, a_ref, w_ref, feat_ref, gf_ref, term_ref, z_ref, cat_ref, acc_ref):
    frames, breadth, channels = feat_ref.shape

    def slab(frame, row):
        if frame < frames:
            return (up_ref, own_ref, down_ref)[row][frame]
        return bnd_ref[row, frame - frames]

    def block(n):
        return slice(n * channels, (n + 1) * channels)

    acc_ref[...] = jnp.zeros_like(acc_ref)
    rows = lax.broadcasted_iota(jnp.int32, (breadth, channels), 0)
    for t in range(frames):
        for j in range(3):
            for i in range(3):
                cat_ref[:, block(i)] = slab(t + 2 - i, 2 - j)
            joined = cat_ref[...]
            part = lax.dot_general(
                joined, w_ref[j], (((1,), (1,)), ((), ())), preferred_element_type=jnp.float32
            )
            if j == 0:
                z_ref[...] = part
            else:
                z_ref[...] += part
            acc_ref[j] += jnp.dot(a_ref[t], joined, preferred_element_type=jnp.float32)
        ahead = pltpu.roll(z_ref[:, block(0)], breadth - 1, 0)
        behind = pltpu.roll(z_ref[:, block(2)], 1, 0)
        grad_input = (
            jnp.where(rows == breadth - 1, 0.0, ahead)
            + z_ref[:, block(1)]
            + jnp.where(rows == 0, 0.0, behind)
        )
        values = feat_ref[t].astype(jnp.float32)
        sigmoid_part = jax.nn.sigmoid(values)
        derivative = sigmoid_part * (1.0 + values * (1.0 - sigmoid_part))
        gf_ref[t] = (own_ref[t].astype(jnp.float32) + derivative * grad_input).astype(gf_ref.dtype)
    for i in range(3):
        for j in range(3):
            term_ref[i * 3 + j] = acc_ref[j, :, block(i)] * factor


def local_grads(pieces, weights, feat, factor):
    frames, breadth, channels = feat.shape
    vmem = pl.BlockSpec(memory_space=pltpu.VMEM)
    params = pltpu.CompilerParams(vmem_limit_bytes=48 * 1024 * 1024)
    a, w = pl.pallas_call(
        prep_kernel,
        out_shape=(
            jax.ShapeDtypeStruct((frames, 3 * channels, breadth), jnp.bfloat16),
            jax.ShapeDtypeStruct((3, 3 * channels, 3 * channels), jnp.bfloat16),
        ),
        in_specs=[vmem] * 2,
        out_specs=(vmem, vmem),
        compiler_params=params,
        cost_estimate=pl.CostEstimate(
            flops=8 * feat.size, bytes_accessed=4 * weights.size + 8 * feat.size, transcendentals=feat.size
        ),
    )(weights, feat)
    operands = tuple(pieces) + (a, w, feat)
    flops = 2 * 2 * frames * 9 * breadth * channels * 3 * channels
    moved = sum(2 * x.size for x in operands) + 2 * feat.size + 4 * 9 * 3 * channels * channels
    return pl.pallas_call(
        lambda *refs: local_kernel(factor, *refs),
        out_shape=(
            jax.ShapeDtypeStruct((frames, breadth, channels), jnp.bfloat16),
            jax.ShapeDtypeStruct((9, 3 * channels, channels), jnp.float32),
        ),
        in_specs=[vmem] * len(operands),
        out_specs=(vmem, vmem),
        scratch_shapes=[
            pltpu.VMEM((breadth, 3 * channels), jnp.float32),
            pltpu.VMEM((breadth, 3 * channels), jnp.bfloat16),
            pltpu.VMEM((3, 3 * channels, 3 * channels), jnp.float32),
        ],
        compiler_params=params,
        cost_estimate=pl.CostEstimate(flops=flops, bytes_accessed=moved, transcendentals=feat.size),
    )(*operands)


def row_neighbours(x, axis):
    count = lax.axis_size(axis)
    up = [(i, i + 1) for i in range(count - 1)]
    down = [(j, i) for i, j in up]
    return lax.ppermute(x, axis, up), lax.ppermute(x, axis, down)


def body(features, cotangent, kernel):
    frames, height, breadth, channels = features.shape
    own = cotangent[:, 0]
    above, below = row_neighbours(own, "ha")
    boundary = passed_along(jnp.stack([above[:2], own[:2], below[:2]]), "ta", -1)
    total_cells = frames * height * breadth * lax.axis_size("ha") * lax.axis_size("ta")
    factor = float(total_cells) ** (-0.5)
    weights = kernel.reshape(-1, channels, channels)
    grad_features, term = local_grads((own, above, below, boundary), weights, features[:, 0], factor)
    term = term.reshape(-1, channels)
    owners = lax.axis_size("ha") * lax.axis_size("ta")
    rows = term.shape[0] // owners
    return (grad_features[:, None], term.reshape(owners, rows * channels)[None])


def physical_mesh(mesh):
    devices = mesh.devices
    coords = np.array([d.coords for d in devices.reshape(-1)])
    sizes = {"x": len(set(coords[:, 0])), "y": len(set(coords[:, 1])), "z": len(set(coords[:, 2]))}
    shape = tuple(sizes[a] for a in PHYSICAL) + (devices.shape[1],)
    grid = devices.reshape(shape)
    flat = np.array([d.coords for d in grid.reshape(-1)]).reshape(shape + (3,))
    want = np.stack(np.meshgrid(*[np.arange(n) for n in shape[:3]], indexing="ij"), -1)
    got = flat[..., 0, :][..., [1, 2, 0]]
    assert (got == want).all()
    return Mesh(grid, PHYSICAL + ("core",))


def reduce_blocks(term, order):
    rows = term.shape[2]
    part = term[0]
    for axis in order:
        count = lax.axis_size(axis)
        shaped = part.reshape((count, part.shape[0] // count) + part.shape[1:])
        part = lax.all_to_all(shaped, axis, 0, 0, tiled=True).sum(0)
    return part[0]


def solution(mesh):
    placed = (P("ta", "ha", None, None), P("ta", "ha", None, None), P())
    local = jax.shard_map(
        body,
        mesh=mesh,
        in_specs=placed,
        out_specs=(P("ta", "ha", None, None), P(("ha", "ta"))),
        check_vma=False,
    )
    grid = physical_mesh(mesh)
    order = ("core", "y", "z", "x")
    stages = ("core", PHYSICAL)
    names = PHYSICAL + ("core",)
    sizes = [grid.shape[a] for a in names]

    def reorder(term):
        n, owners = term.shape[:2]
        t = term.reshape((n,) + tuple(sizes) + term.shape[2:])
        perm = [0] + [1 + names.index(a) for a in order] + list(range(5, t.ndim))
        return t.transpose(perm).reshape(term.shape)

    def reduce_fn(term):
        rows = 27
        return reduce_blocks(term, order)

    rows_per = None

    def run(features, cotangent, kernel):
        grad_features, term = local(features, cotangent, kernel)
        channels = kernel.shape[-1]
        owners = term.shape[1]
        taps_rows = kernel.shape[0] * kernel.shape[1] * kernel.shape[2] * kernel.shape[3]
        rows = taps_rows // owners
        term = reorder(term)
        spec = P(names)
        part = jax.shard_map(
            lambda t: reduce_blocks(t, stages).reshape(rows, channels),
            mesh=grid,
            in_specs=spec,
            out_specs=P(names),
            check_vma=False,
        )(term)
        part = lax.with_sharding_constraint(part, NamedSharding(mesh, P(("ha", "ta"), None)))
        return grad_features, part

    return run
```
